512 devices in a mesh: rows: 64 (over x_hi, z, core), chan: 8 (over x_lo, y).
Axes of the slice: x: 4 (x_hi: 2, x_lo: 2; x = x_hi * 2 + x_lo), y: 4, z: 16, core: 2. Of those that a mesh axis runs over, the one named last changes fastest.
Arguments:
- hidden: float32 [32, 2048, 2048], P('chan', 'rows'), may hold values from -6 to 6
- front: float32 [2048, 2048], P('rows', 'chan'), may hold values from -6 to 6
- spectral_weight: float32 [2, 128, 128, 32, 32], P(None, 'rows', 'chan'), may hold values from -0.5 to 0.5
- skip_gain: float32 [32], P('chan'), may hold values from 0.5 to 1.5
- skip_bias: float32 [32], P('chan'), may hold values from -3 to 3
- project_weight: float32 [2, 32], P(None, 'chan'), may hold values from -1 to 1
- project_bias: float32 [2], replicated, may hold values from -3 to 3
- ice_mask: int32 [2048, 2048], P('rows', 'chan'), may hold values 0 or 1
- front_flags: int32 [2048, 2048], P('rows', 'chan'), may hold values 0 or 1
Outputs:
- velocity: float32 [2, 2048, 2048], P(None, 'rows', 'chan')
- front_next: float32 [2048, 2048], P('rows', 'chan')
The draws below stay inside these ranges and needn't reach their ends.
All inputs are finite; a program needn't handle non-finite values. No bound on the sum of `ice_mask` or of `front_flags` on one device may be relied on, other than what follows from the above.
Results may differ from the reference program's by a relative error of at most 0.0003.
Values sent between devices are 32-bit elements; how exact they have to be, the bound alone decides.
No kernel may reach another device: no remote copies, remote signals or barrier semaphores. Data moves between devices by JAX's collectives and lax.ppermute only.
A program may use at most 128 MiB of HBM per device.

```python
import math
import jax
import jax.numpy as jnp
from jax import lax

C = 32
MX = 128
MY = 128
NY = 2048
LS_STEPS = 4
NX = 2048


def set_ends(result, rng, smallest, high):
    index_at = [jax.random.randint(jax.random.fold_in(rng, axis), (), 0, length) for axis, length in enumerate(result.shape)]
    main_axis = result.shape.index(max(result.shape))
    neighbour = index_at[:main_axis] + [(index_at[main_axis] + 1) % result.shape[main_axis]] + index_at[main_axis + 1:]
    return result.at[tuple(index_at)].set(smallest).at[tuple(neighbour)].set(high)


def block_levels(rng, dims, shards, low, top_value):
    level = 1.0
    for dim, parts in shards:
        heights = jax.random.uniform(jax.random.fold_in(jax.random.fold_in(rng, 6), dim), (parts,), jnp.float32, low / len(shards), top_value / len(shards))
        level = level * jnp.repeat(jnp.exp(heights), dims[dim] // parts).reshape((-1,) + (1,) * (len(dims) - 1 - dim))
    return level


def normal_values(stream_key, dims, spread, reach, split=(), held_as=jnp.bfloat16):
    level = block_levels(stream_key, dims, split, -0.22, 0.18) if split else 1.0
    entries = jax.random.normal(stream_key, dims, jnp.float32) * spread * level
    return jnp.minimum(jnp.maximum(entries, -reach), reach).astype(held_as)


def setup_inputs(seed: int = 0) -> dict:
    keys = jax.random.split(jax.random.key(seed), 10)
    hidden = normal_values(keys[0], (C, NX, NY), 1.0, 6.0, ((0, 8), (1, 64)), jnp.float32)
    front = normal_values(keys[1], (NX, NY), 1.0, 6.0, ((0, 64), (1, 8)), jnp.float32)
    spectral_weight = normal_values(keys[2], (2, MY, MX, C, C), (4 * C) ** -0.5, 0.5, ((1, 64), (2, 8)), jnp.float32)
    skip_gain = jnp.clip(1.0 + 0.1 * jax.random.normal(keys[3], (C,), jnp.float32), 0.5, 1.5)
    skip_bias = normal_values(keys[4], (C,), 0.5, 3.0, ((0, 8),), jnp.float32)
    project_weight = normal_values(keys[5], (2, C), C ** -0.5, 1.0, ((1, 8),), jnp.float32)
    project_bias = normal_values(keys[6], (2,), 0.5, 3.0, (), jnp.float32)
    ice_mask = set_ends((jax.random.randint(keys[7], (NX, NY), 0, 4) < 3).astype(jnp.int32), jax.random.fold_in(keys[7], 1), 0, 1)
    front_flags = set_ends((jax.random.randint(keys[8], (NX, NY), 0, 2) < 1).astype(jnp.int32), jax.random.fold_in(keys[8], 1), 0, 1)
    return {"hidden": hidden, "front": front, "spectral_weight": spectral_weight, "skip_gain": skip_gain, "skip_bias": skip_bias, "project_weight": project_weight, "project_bias": project_bias, "ice_mask": ice_mask, "front_flags": front_flags}


time_step = 0.25

def advance(padded, speed_x, speed_y, band):
    center = padded[1:-1, 1:-1]
    back_x = center - padded[:-2, 1:-1]
    ahead_x = padded[2:, 1:-1] - center
    back_y = center - padded[1:-1, :-2]
    ahead_y = padded[1:-1, 2:] - center
    transport = jnp.maximum(speed_x, 0.0) * back_x + jnp.minimum(speed_x, 0.0) * ahead_x
    transport = transport + jnp.maximum(speed_y, 0.0) * back_y + jnp.minimum(speed_y, 0.0) * ahead_y
    return center - time_step * band * transport

def reference(hidden, front, spectral_weight, skip_gain, skip_bias, project_weight, project_bias, ice_mask, front_flags):
    highest = lax.Precision.HIGHEST
    half_modes = MX // 2
    spec_y = jnp.fft.rfft(hidden, axis=2)[:, :, :MY]
    spec_full = jnp.fft.fft(spec_y, axis=1)
    kept = jnp.concatenate([spec_full[:, :half_modes], spec_full[:, NX - half_modes:]], axis=1)
    complex_weight = spectral_weight[0] + 1j * spectral_weight[1]
    mixed = jnp.einsum('qpio,ipq->opq', complex_weight, kept, precision=highest)
    placed = jnp.zeros((C, NX, MY), mixed.dtype)
    placed = placed.at[:, :half_modes].set(mixed[:, :half_modes])
    placed = placed.at[:, NX - half_modes:].set(mixed[:, half_modes:])
    spectral = jnp.fft.irfft(jnp.fft.ifft(placed, axis=1), n=NY, axis=2)
    spectral = spectral * math.sqrt(NX * NY / (MX * MY))
    activated = jax.nn.gelu(spectral + skip_gain[:, None, None] * hidden + skip_bias[:, None, None], approximate=False)
    velocity = jnp.einsum('jc,cxy->jxy', project_weight, activated, precision=highest) + project_bias[:, None, None]
    velocity = velocity * ice_mask.astype(jnp.float32)[None]
    band = front_flags.astype(jnp.float32)
    level = front
    for level_step in range(LS_STEPS):
        level = advance(jnp.pad(level, 1), velocity[0], velocity[1], band)
    return (velocity, level)
```

```python
import math

import jax
import jax.numpy as jnp
from jax import lax
from jax.sharding import PartitionSpec as P

LS_STEPS = 4


time_step = 0.25
highest = lax.Precision.HIGHEST


def with_halo(block, sides, width):
    for axis, dim in sides:
        count = lax.axis_size(axis)
        forward = [(i, i + 1) for i in range(count - 1)]
        backward = [(target, source) for source, target in forward]
        low = lax.ppermute(
            lax.slice_in_dim(block, block.shape[dim] - width, None, axis=dim), axis, forward
        )
        high = lax.ppermute(lax.slice_in_dim(block, 0, width, axis=dim), axis, backward)
        block = jnp.concatenate([low, block, high], axis=dim)
    return block


def angles(freqs, places, length):
    product = freqs[:, None] * places[None, :] % length
    return 2.0 * math.pi / length * product.astype(jnp.float32)


def x_tables(total_modes, places, length):
    mode_ids = jnp.arange(total_modes, dtype=jnp.int32)
    wave_ids = mode_ids - total_modes * (mode_ids >= total_modes // 2).astype(jnp.int32)
    phase = angles(wave_ids, places, length)
    return jnp.stack([jnp.cos(phase), jnp.sin(phase)])


def forward_x(spectra, tables):
    parts = jnp.einsum("cqrx,spx->cqrsp", spectra, tables, precision=highest)
    real_part = parts[:, :, 0, 0] + parts[:, :, 1, 1]
    imag_part = parts[:, :, 1, 0] - parts[:, :, 0, 1]
    return jnp.stack([real_part, imag_part], axis=2)


def inverse_x(spectra, tables):
    parts = jnp.einsum("cqrp,spx->cqrsx", spectra, tables, precision=highest)
    real_part = parts[:, :, 0, 0] - parts[:, :, 1, 1]
    imag_part = parts[:, :, 0, 1] + parts[:, :, 1, 0]
    return jnp.stack([real_part, imag_part], axis=2)


def windows(block, count, size, halo):
    padded = jnp.pad(block, [(0, 0)] * (block.ndim - 1) + [(halo, size)])
    lead = block.shape[:-1]
    main = padded[..., : count * size].reshape(lead + (count, size))
    tail = padded[..., size : size + count * size].reshape(lead + (count, size))
    return jnp.concatenate([main, tail[..., : 2 * halo]], axis=-1)


def advance(padded, speed_x, speed_y, band):
    center = padded[1:-1, 1:-1]
    back_x = center - padded[:-2, 1:-1]
    ahead_x = padded[2:, 1:-1] - center
    back_y = center - padded[1:-1, :-2]
    ahead_y = padded[1:-1, 2:] - center
    transport = jnp.maximum(speed_x, 0.0) * back_x + jnp.minimum(speed_x, 0.0) * ahead_x
    transport = transport + jnp.maximum(speed_y, 0.0) * back_y + jnp.minimum(speed_y, 0.0) * ahead_y
    return center - time_step * band * transport


def on_device(
    hidden,
    front,
    spectral_weight,
    skip_gain,
    skip_bias,
    project_weight,
    project_bias,
    ice_mask,
    front_flags,
):
    halo = LS_STEPS
    local_chan, row_count, columns = hidden.shape
    row_devices = lax.axis_size("rows")
    chan_devices = lax.axis_size("chan")
    local_ymodes = spectral_weight.shape[1]
    all_rows = row_count * row_devices
    all_xmodes = spectral_weight.shape[2] * chan_devices
    all_ymodes = local_ymodes * row_devices
    tile_cols = columns // chan_devices
    win_rows = row_count + 2 * halo
    norm_scale = 1.0 / math.sqrt(all_rows * columns * all_xmodes * all_ymodes)

    fields = jnp.stack(
        [front, front_flags.astype(jnp.float32), ice_mask.astype(jnp.float32)]
    )
    fields = with_halo(fields, (("rows", 1), ("chan", 2)), halo)
    hidden_win = with_halo(hidden, (("rows", 1),), halo)

    y_ids = jnp.arange(all_ymodes, dtype=jnp.int32)
    y_phase = angles(y_ids, jnp.arange(columns, dtype=jnp.int32), columns)
    forward_y = jnp.stack([jnp.cos(y_phase), -jnp.sin(y_phase)], axis=1).reshape(
        2 * all_ymodes, columns
    )
    y_weights = jnp.where(y_ids == 0, 1.0, 2.0).astype(jnp.float32)[:, None] * norm_scale
    inverse_y = jnp.stack(
        [y_weights * jnp.cos(y_phase), -y_weights * jnp.sin(y_phase)], axis=1
    ).reshape(2 * all_ymodes, columns)

    spec_y = jnp.einsum("cxy,ky->ckx", hidden, forward_y, precision=highest)
    by_freq = lax.all_to_all(spec_y, "rows", split_axis=1, concat_axis=2, tiled=True)
    by_freq = by_freq.reshape(local_chan, local_ymodes, 2, all_rows)
    all_x = jnp.arange(all_rows, dtype=jnp.int32)
    spectra = forward_x(by_freq, x_tables(all_xmodes, all_x, all_rows))

    gathered = lax.all_to_all(spectra, "chan", split_axis=3, concat_axis=0, tiled=True)
    real_in = gathered[:, :, 0]
    imag_in = gathered[:, :, 1]
    real_out = jnp.einsum(
        "qpio,iqp->oqp", spectral_weight[0], real_in, precision=highest
    ) - jnp.einsum("qpio,iqp->oqp", spectral_weight[1], imag_in, precision=highest)
    imag_out = jnp.einsum(
        "qpio,iqp->oqp", spectral_weight[0], imag_in, precision=highest
    ) + jnp.einsum("qpio,iqp->oqp", spectral_weight[1], real_in, precision=highest)
    mixed = lax.all_to_all(
        jnp.stack([real_out, imag_out], axis=2), "chan", split_axis=0, concat_axis=3, tiled=True
    )

    starts = jnp.arange(row_devices, dtype=jnp.int32)[:, None] * row_count - halo
    places = (starts + jnp.arange(win_rows, dtype=jnp.int32)[None, :]).reshape(-1) % all_rows
    inverted = inverse_x(mixed, x_tables(all_xmodes, places, all_rows))
    inverted = inverted.reshape(local_chan, local_ymodes, 2, row_devices, win_rows)
    inverted = lax.all_to_all(inverted, "rows", split_axis=3, concat_axis=1, tiled=True)
    inverted = inverted.reshape(local_chan, 2 * all_ymodes, win_rows)

    spectral = jnp.einsum("ckx,ky->cxy", inverted, inverse_y, precision=highest)
    activated = jax.nn.gelu(
        spectral + skip_gain[:, None, None] * hidden_win + skip_bias[:, None, None],
        approximate=False,
    )
    partial_speed = jnp.einsum("jc,cxy->jxy", project_weight, activated, precision=highest)
    sent = windows(partial_speed, chan_devices, tile_cols, halo)
    received = lax.all_to_all(sent, "chan", split_axis=2, concat_axis=2, tiled=True)
    speed = jnp.sum(received, axis=2) + project_bias[:, None, None]
    speed = speed * fields[2][None]
    velocity = speed[:, halo : halo + row_count, halo : halo + tile_cols]

    level = fields[0]
    band = fields[1]
    for level_step in range(LS_STEPS):
        inner = level_step + 1
        rows_end = win_rows - inner
        cols_end = tile_cols + 2 * halo - inner
        level = advance(
            level,
            speed[0, inner:rows_end, inner:cols_end],
            speed[1, inner:rows_end, inner:cols_end],
            band[inner:rows_end, inner:cols_end],
        )
    return (velocity, level)


def solution(mesh):
    return jax.shard_map(
        on_device,
        mesh=mesh,
        in_specs=(
            P("chan", "rows", None),
            P("rows", "chan"),
            P(None, "rows", "chan", None, None),
            P("chan"),
            P("chan"),
            P(None, "chan"),
            P(),
            P("rows", "chan"),
            P("rows", "chan"),
        ),
        out_specs=(P(None, "rows", "chan"), P("rows", "chan")),
        check_vma=False,
    )
```

```python
import math

import jax
import jax.numpy as jnp
from jax import lax
from jax.sharding import PartitionSpec as P

LS_STEPS = 4


time_step = 0.25
highest = lax.Precision.HIGHEST


def with_halo(block, sides, width):
    for axis, dim in sides:
        count = lax.axis_size(axis)
        forward = [(i, i + 1) for i in range(count - 1)]
        backward = [(target, source) for source, target in forward]
        low = lax.ppermute(
            lax.slice_in_dim(block, block.shape[dim] - width, None, axis=dim), axis, forward
        )
        high = lax.ppermute(lax.slice_in_dim(block, 0, width, axis=dim), axis, backward)
        block = jnp.concatenate([low, block, high], axis=dim)
    return block


def angles(freqs, places, length):
    product = freqs[:, None] * places[None, :] % length
    return 2.0 * math.pi / length * product.astype(jnp.float32)


def base_table(modes, length):
    phase = angles(jnp.arange(modes, dtype=jnp.int32), jnp.arange(length, dtype=jnp.int32), length)
    return jnp.concatenate([jnp.cos(phase), -jnp.sin(phase)])


def fold_modes(vec, half):
    pos = jnp.pad(vec[..., :half], [(0, 0)] * (vec.ndim - 1) + [(0, 1)])
    neg = jnp.pad(jnp.flip(vec[..., half:], -1), [(0, 0)] * (vec.ndim - 1) + [(1, 0)])
    return pos, neg


def unfold_modes(plus, minus, half):
    return jnp.concatenate([plus[..., :half], jnp.flip(minus[..., 1 : half + 1], -1)], axis=-1)


def windows(block, count, size, halo):
    padded = jnp.pad(block, [(0, 0)] * (block.ndim - 1) + [(halo, size)])
    lead = block.shape[:-1]
    main = padded[..., : count * size].reshape(lead + (count, size))
    tail = padded[..., size : size + count * size].reshape(lead + (count, size))
    return jnp.concatenate([main, tail[..., : 2 * halo]], axis=-1)


def halo_2d(block, width):
    n_rows = lax.axis_size("rows")
    n_chan = lax.axis_size("chan")

    def shifted(piece, d_row, d_chan):
        pairs = [
            (r * n_chan + c, (r + d_row) * n_chan + c + d_chan)
            for r in range(n_rows)
            for c in range(n_chan)
            if 0 <= r + d_row < n_rows and 0 <= c + d_chan < n_chan
        ]
        return lax.ppermute(piece, ("rows", "chan"), pairs)

    lo, hi = slice(-width, None), slice(0, width)
    every = slice(None)
    parts = {}
    for d_row, rows in ((1, lo), (0, every), (-1, hi)):
        for d_chan, cols in ((1, lo), (0, every), (-1, hi)):
            piece = block[..., rows, cols]
            parts[d_row, d_chan] = piece if d_row == d_chan == 0 else shifted(piece, d_row, d_chan)
    bands = [
        jnp.concatenate([parts[d_row, 1], parts[d_row, 0], parts[d_row, -1]], axis=-1)
        for d_row in (1, 0, -1)
    ]
    return jnp.concatenate(bands, axis=-2)


def advance(padded, speed_x, speed_y, band):
    center = padded[1:-1, 1:-1]
    back_x = center - padded[:-2, 1:-1]
    ahead_x = padded[2:, 1:-1] - center
    back_y = center - padded[1:-1, :-2]
    ahead_y = padded[1:-1, 2:] - center
    transport = jnp.maximum(speed_x, 0.0) * back_x + jnp.minimum(speed_x, 0.0) * ahead_x
    transport = transport + jnp.maximum(speed_y, 0.0) * back_y + jnp.minimum(speed_y, 0.0) * ahead_y
    return center - time_step * band * transport


def on_device(
    hidden,
    front,
    spectral_weight,
    skip_gain,
    skip_bias,
    project_weight,
    project_bias,
    ice_mask,
    front_flags,
):
    halo = LS_STEPS
    local_chan, row_count, columns = hidden.shape
    row_devices = lax.axis_size("rows")
    chan_devices = lax.axis_size("chan")
    local_ymodes = spectral_weight.shape[1]
    all_rows = row_count * row_devices
    all_xmodes = spectral_weight.shape[2] * chan_devices
    all_ymodes = local_ymodes * row_devices
    tile_cols = columns // chan_devices
    win_rows = row_count + 2 * halo
    norm_scale = 1.0 / math.sqrt(all_rows * columns * all_xmodes * all_ymodes)

    fields = jnp.stack(
        [front, front_flags.astype(jnp.float32), ice_mask.astype(jnp.float32)]
    )
    fields = halo_2d(fields, halo)
    hidden_win = with_halo(hidden, (("rows", 1),), halo)

    table = base_table(all_ymodes, columns)
    half = all_xmodes // 2
    if all_rows == columns and all_ymodes > half:
        x_table = table
    else:
        x_table = base_table(half + 1, all_rows)
    x_modes = x_table.shape[0] // 2

    spec_y = jnp.einsum("cxy,ky->ckx", hidden, table, precision=highest)
    spec_y = spec_y.reshape(local_chan, 2, all_ymodes, row_count)
    by_freq = lax.all_to_all(spec_y, "rows", split_axis=2, concat_axis=3, tiled=True)
    parts = jnp.einsum("caqx,kx->caqk", by_freq, x_table, precision=highest)
    cos_part = parts[..., :x_modes]
    sin_part = parts[..., x_modes:]
    real_in = unfold_modes(
        cos_part[:, 0] - sin_part[:, 1], cos_part[:, 0] + sin_part[:, 1], half
    )
    imag_in = unfold_modes(
        cos_part[:, 1] + sin_part[:, 0], cos_part[:, 1] - sin_part[:, 0], half
    )
    spectra = jnp.stack([real_in, imag_in], axis=2)

    gathered = lax.all_to_all(spectra, "chan", split_axis=3, concat_axis=0, tiled=True)
    real_in = gathered[:, :, 0]
    imag_in = gathered[:, :, 1]
    real_out = jnp.einsum(
        "qpio,iqp->oqp", spectral_weight[0], real_in, precision=highest
    ) - jnp.einsum("qpio,iqp->oqp", spectral_weight[1], imag_in, precision=highest)
    imag_out = jnp.einsum(
        "qpio,iqp->oqp", spectral_weight[0], imag_in, precision=highest
    ) + jnp.einsum("qpio,iqp->oqp", spectral_weight[1], real_in, precision=highest)
    mixed = lax.all_to_all(
        jnp.stack([real_out, imag_out], axis=2), "chan", split_axis=0, concat_axis=3, tiled=True
    )

    real_pos, real_neg = fold_modes(mixed[:, :, 0], half)
    imag_pos, imag_neg = fold_modes(mixed[:, :, 1], half)
    pad = [(0, 0), (0, 0), (0, x_modes - half - 1)]
    coef_real = jnp.concatenate(
        [jnp.pad(real_pos + real_neg, pad), jnp.pad(imag_pos - imag_neg, pad)], axis=-1
    )
    coef_imag = jnp.concatenate(
        [jnp.pad(imag_pos + imag_neg, pad), jnp.pad(real_neg - real_pos, pad)], axis=-1
    )
    coef = jnp.stack([coef_real, coef_imag], axis=1)
    inverted = jnp.einsum("otqk,kx->otqx", coef, x_table, precision=highest)
    inverted = windows(inverted, row_devices, row_count, halo)
    inverted = lax.all_to_all(inverted, "rows", split_axis=3, concat_axis=2, tiled=True)
    y_weights = jnp.where(jnp.arange(all_ymodes) == 0, 1.0, 2.0).astype(jnp.float32) * norm_scale
    inverted = inverted.reshape(local_chan, 2, all_ymodes, win_rows) * y_weights[:, None]
    inverted = inverted.reshape(local_chan, 2 * all_ymodes, win_rows)

    spectral = jnp.einsum("ckx,ky->cxy", inverted, table, precision=highest)
    activated = jax.nn.gelu(
        spectral + skip_gain[:, None, None] * hidden_win + skip_bias[:, None, None],
        approximate=False,
    )
    partial_speed = jnp.einsum("jc,cxy->jxy", project_weight, activated, precision=highest)
    sent = windows(partial_speed, chan_devices, tile_cols, halo)
    received = lax.all_to_all(sent, "chan", split_axis=2, concat_axis=2, tiled=True)
    speed = jnp.sum(received, axis=2) + project_bias[:, None, None]
    speed = speed * fields[2][None]
    velocity = speed[:, halo : halo + row_count, halo : halo + tile_cols]

    level = fields[0]
    band = fields[1]
    for level_step in range(LS_STEPS):
        inner = level_step + 1
        rows_end = win_rows - inner
        cols_end = tile_cols + 2 * halo - inner
        level = advance(
            level,
            speed[0, inner:rows_end, inner:cols_end],
            speed[1, inner:rows_end, inner:cols_end],
            band[inner:rows_end, inner:cols_end],
        )
    return (velocity, level)


def solution(mesh):
    return jax.shard_map(
        on_device,
        mesh=mesh,
        in_specs=(
            P("chan", "rows", None),
            P("rows", "chan"),
            P(None, "rows", "chan", None, None),
            P("chan"),
            P("chan"),
            P(None, "chan"),
            P(),
            P("rows", "chan"),
            P("rows", "chan"),
        ),
        out_specs=(P(None, "rows", "chan"), P("rows", "chan")),
        check_vma=False,
    )
```

```python
import math

import jax
import jax.numpy as jnp
from jax import lax
from jax.sharding import PartitionSpec as P

LS_STEPS = 4


time_step = 0.25
highest = lax.Precision.HIGHEST


def with_halo(block, sides, width):
    for axis, dim in sides:
        count = lax.axis_size(axis)
        forward = [(i, i + 1) for i in range(count - 1)]
        backward = [(target, source) for source, target in forward]
        low = lax.ppermute(
            lax.slice_in_dim(block, block.shape[dim] - width, None, axis=dim), axis, forward
        )
        high = lax.ppermute(lax.slice_in_dim(block, 0, width, axis=dim), axis, backward)
        block = jnp.concatenate([low, block, high], axis=dim)
    return block


def angles(freqs, places, length):
    product = freqs[:, None] * places[None, :] % length
    return 2.0 * math.pi / length * product.astype(jnp.float32)


def base_table(modes, length):
    phase = angles(jnp.arange(modes, dtype=jnp.int32), jnp.arange(length, dtype=jnp.int32), length)
    return jnp.concatenate([jnp.cos(phase), -jnp.sin(phase)])


def fold_modes(vec, half):
    pos = jnp.pad(vec[..., :half], [(0, 0)] * (vec.ndim - 1) + [(0, 1)])
    neg = jnp.pad(jnp.flip(vec[..., half:], -1), [(0, 0)] * (vec.ndim - 1) + [(1, 0)])
    return pos, neg


def unfold_modes(plus, minus, half):
    return jnp.concatenate([plus[..., :half], jnp.flip(minus[..., 1 : half + 1], -1)], axis=-1)


def windows(block, count, size, halo):
    padded = jnp.pad(block, [(0, 0)] * (block.ndim - 1) + [(halo, size)])
    lead = block.shape[:-1]
    main = padded[..., : count * size].reshape(lead + (count, size))
    tail = padded[..., size : size + count * size].reshape(lead + (count, size))
    return jnp.concatenate([main, tail[..., : 2 * halo]], axis=-1)


def halo_2d(block, width):
    n_rows = lax.axis_size("rows")
    n_chan = lax.axis_size("chan")

    def shifted(piece, d_row, d_chan):
        pairs = [
            (r * n_chan + c, (r + d_row) * n_chan + c + d_chan)
            for r in range(n_rows)
            for c in range(n_chan)
            if 0 <= r + d_row < n_rows and 0 <= c + d_chan < n_chan
        ]
        return lax.ppermute(piece, ("rows", "chan"), pairs)

    lo, hi = slice(-width, None), slice(0, width)
    every = slice(None)
    parts = {}
    for d_row, rows in ((1, lo), (0, every), (-1, hi)):
        for d_chan, cols in ((1, lo), (0, every), (-1, hi)):
            piece = block[..., rows, cols]
            parts[d_row, d_chan] = piece if d_row == d_chan == 0 else shifted(piece, d_row, d_chan)
    bands = [
        jnp.concatenate([parts[d_row, 1], parts[d_row, 0], parts[d_row, -1]], axis=-1)
        for d_row in (1, 0, -1)
    ]
    return jnp.concatenate(bands, axis=-2)


def rows_halo_pair(first, second, width):
    count = lax.axis_size("rows")
    forward = [(i, i + 1) for i in range(count - 1)]
    backward = [(target, source) for source, target in forward]

    def packed(rows):
        a, b = first[..., rows, :], second[..., rows, :]
        return jnp.concatenate([a.reshape(-1), b.reshape(-1)]), a.shape, b.shape

    def unpacked(flat, a_shape, b_shape):
        split = math.prod(a_shape)
        return flat[:split].reshape(a_shape), flat[split:].reshape(b_shape)

    low, a_shape, b_shape = packed(slice(-width, None))
    high, _, _ = packed(slice(0, width))
    low_a, low_b = unpacked(lax.ppermute(low, "rows", forward), a_shape, b_shape)
    high_a, high_b = unpacked(lax.ppermute(high, "rows", backward), a_shape, b_shape)
    return (
        jnp.concatenate([low_a, first, high_a], axis=-2),
        jnp.concatenate([low_b, second, high_b], axis=-2),
    )


def advance(padded, speed_x, speed_y, band):
    center = padded[1:-1, 1:-1]
    back_x = center - padded[:-2, 1:-1]
    ahead_x = padded[2:, 1:-1] - center
    back_y = center - padded[1:-1, :-2]
    ahead_y = padded[1:-1, 2:] - center
    transport = jnp.maximum(speed_x, 0.0) * back_x + jnp.minimum(speed_x, 0.0) * ahead_x
    transport = transport + jnp.maximum(speed_y, 0.0) * back_y + jnp.minimum(speed_y, 0.0) * ahead_y
    return center - time_step * band * transport


def on_device(
    hidden,
    front,
    spectral_weight,
    skip_gain,
    skip_bias,
    project_weight,
    project_bias,
    ice_mask,
    front_flags,
):
    halo = LS_STEPS
    local_chan, row_count, columns = hidden.shape
    row_devices = lax.axis_size("rows")
    chan_devices = lax.axis_size("chan")
    local_ymodes = spectral_weight.shape[1]
    all_rows = row_count * row_devices
    all_xmodes = spectral_weight.shape[2] * chan_devices
    all_ymodes = local_ymodes * row_devices
    tile_cols = columns // chan_devices
    win_rows = row_count + 2 * halo
    norm_scale = 1.0 / math.sqrt(all_rows * columns * all_xmodes * all_ymodes)

    fields = jnp.stack(
        [front, front_flags.astype(jnp.float32), ice_mask.astype(jnp.float32)]
    )
    hidden_win, fields = rows_halo_pair(hidden, fields, halo)
    fields = with_halo(fields, (("chan", 2),), halo)
    fields, hidden_win = lax.optimization_barrier((fields, hidden_win))

    table = base_table(all_ymodes, columns)
    half = all_xmodes // 2
    if all_rows == columns and all_ymodes > half:
        x_table = table
    else:
        x_table = base_table(half + 1, all_rows)
    x_modes = x_table.shape[0] // 2

    spec_y = jnp.einsum("cxy,ky->ckx", hidden, table, precision=highest)
    spec_y = spec_y.reshape(local_chan, 2, all_ymodes, row_count)
    by_freq = lax.all_to_all(spec_y, "rows", split_axis=2, concat_axis=3, tiled=True)
    parts = jnp.einsum("caqx,kx->caqk", by_freq, x_table, precision=highest)
    cos_part = parts[..., :x_modes]
    sin_part = parts[..., x_modes:]
    real_in = unfold_modes(
        cos_part[:, 0] - sin_part[:, 1], cos_part[:, 0] + sin_part[:, 1], half
    )
    imag_in = unfold_modes(
        cos_part[:, 1] + sin_part[:, 0], cos_part[:, 1] - sin_part[:, 0], half
    )
    spectra = jnp.stack([real_in, imag_in], axis=2)

    gathered = lax.all_to_all(spectra, "chan", split_axis=3, concat_axis=0, tiled=True)
    real_in = gathered[:, :, 0]
    imag_in = gathered[:, :, 1]
    real_out = jnp.einsum(
        "qpio,iqp->oqp", spectral_weight[0], real_in, precision=highest
    ) - jnp.einsum("qpio,iqp->oqp", spectral_weight[1], imag_in, precision=highest)
    imag_out = jnp.einsum(
        "qpio,iqp->oqp", spectral_weight[0], imag_in, precision=highest
    ) + jnp.einsum("qpio,iqp->oqp", spectral_weight[1], real_in, precision=highest)
    mixed = lax.all_to_all(
        jnp.stack([real_out, imag_out], axis=2), "chan", split_axis=0, concat_axis=3, tiled=True
    )

    real_pos, real_neg = fold_modes(mixed[:, :, 0], half)
    imag_pos, imag_neg = fold_modes(mixed[:, :, 1], half)
    pad = [(0, 0), (0, 0), (0, x_modes - half - 1)]
    coef_real = jnp.concatenate(
        [jnp.pad(real_pos + real_neg, pad), jnp.pad(imag_pos - imag_neg, pad)], axis=-1
    )
    coef_imag = jnp.concatenate(
        [jnp.pad(imag_pos + imag_neg, pad), jnp.pad(real_neg - real_pos, pad)], axis=-1
    )
    coef = jnp.stack([coef_real, coef_imag], axis=1)
    inverted = jnp.einsum("otqk,kx->otqx", coef, x_table, precision=highest)
    inverted = windows(inverted, row_devices, row_count, halo)
    inverted = lax.all_to_all(inverted, "rows", split_axis=3, concat_axis=2, tiled=True)
    y_weights = jnp.where(jnp.arange(all_ymodes) == 0, 1.0, 2.0).astype(jnp.float32) * norm_scale
    inverted = inverted.reshape(local_chan, 2, all_ymodes, win_rows) * y_weights[:, None]
    inverted = inverted.reshape(local_chan, 2 * all_ymodes, win_rows)

    spectral = jnp.einsum("ckx,ky->cxy", inverted, table, precision=highest)
    activated = jax.nn.gelu(
        spectral + skip_gain[:, None, None] * hidden_win + skip_bias[:, None, None],
        approximate=False,
    )
    partial_speed = jnp.einsum("jc,cxy->jxy", project_weight, activated, precision=highest)
    sent = windows(partial_speed, chan_devices, tile_cols, halo)
    received = lax.all_to_all(sent, "chan", split_axis=2, concat_axis=2, tiled=True)
    speed = jnp.sum(received, axis=2) + project_bias[:, None, None]
    speed = speed * fields[2][None]
    velocity = speed[:, halo : halo + row_count, halo : halo + tile_cols]

    level = fields[0]
    band = fields[1]
    for level_step in range(LS_STEPS):
        inner = level_step + 1
        rows_end = win_rows - inner
        cols_end = tile_cols + 2 * halo - inner
        level = advance(
            level,
            speed[0, inner:rows_end, inner:cols_end],
            speed[1, inner:rows_end, inner:cols_end],
            band[inner:rows_end, inner:cols_end],
        )
    return (velocity, level)


def solution(mesh):
    return jax.shard_map(
        on_device,
        mesh=mesh,
        in_specs=(
            P("chan", "rows", None),
            P("rows", "chan"),
            P(None, "rows", "chan", None, None),
            P("chan"),
            P("chan"),
            P(None, "chan"),
            P(),
            P("rows", "chan"),
            P("rows", "chan"),
        ),
        out_specs=(P(None, "rows", "chan"), P("rows", "chan")),
        check_vma=False,
    )
```

```python
import math

import jax
import jax.numpy as jnp
from jax import lax
from jax.sharding import PartitionSpec as P

LS_STEPS = 4


time_step = 0.25
highest = lax.Precision.HIGHEST


def with_halo(block, sides, width):
    for axis, dim in sides:
        count = lax.axis_size(axis)
        forward = [(i, i + 1) for i in range(count - 1)]
        backward = [(target, source) for source, target in forward]
        low = lax.ppermute(
            lax.slice_in_dim(block, block.shape[dim] - width, None, axis=dim), axis, forward
        )
        high = lax.ppermute(lax.slice_in_dim(block, 0, width, axis=dim), axis, backward)
        block = jnp.concatenate([low, block, high], axis=dim)
    return block


def angles(freqs, places, length):
    product = freqs[:, None] * places[None, :] % length
    return 2.0 * math.pi / length * product.astype(jnp.float32)


def base_table(modes, length):
    phase = angles(jnp.arange(modes, dtype=jnp.int32), jnp.arange(length, dtype=jnp.int32), length)
    return jnp.concatenate([jnp.cos(phase), -jnp.sin(phase)])


def fold_modes(vec, half):
    pos = jnp.pad(vec[..., :half], [(0, 0)] * (vec.ndim - 1) + [(0, 1)])
    neg = jnp.pad(jnp.flip(vec[..., half:], -1), [(0, 0)] * (vec.ndim - 1) + [(1, 0)])
    return pos, neg


def unfold_modes(plus, minus, half):
    return jnp.concatenate([plus[..., :half], jnp.flip(minus[..., 1 : half + 1], -1)], axis=-1)


def windows(block, count, size, halo):
    padded = jnp.pad(block, [(0, 0)] * (block.ndim - 1) + [(halo, size)])
    lead = block.shape[:-1]
    main = padded[..., : count * size].reshape(lead + (count, size))
    tail = padded[..., size : size + count * size].reshape(lead + (count, size))
    return jnp.concatenate([main, tail[..., : 2 * halo]], axis=-1)


def halo_2d(block, width):
    n_rows = lax.axis_size("rows")
    n_chan = lax.axis_size("chan")

    def shifted(piece, d_row, d_chan):
        pairs = [
            (r * n_chan + c, (r + d_row) * n_chan + c + d_chan)
            for r in range(n_rows)
            for c in range(n_chan)
            if 0 <= r + d_row < n_rows and 0 <= c + d_chan < n_chan
        ]
        return lax.ppermute(piece, ("rows", "chan"), pairs)

    lo, hi = slice(-width, None), slice(0, width)
    every = slice(None)
    parts = {}
    for d_row, rows in ((1, lo), (0, every), (-1, hi)):
        for d_chan, cols in ((1, lo), (0, every), (-1, hi)):
            piece = block[..., rows, cols]
            parts[d_row, d_chan] = piece if d_row == d_chan == 0 else shifted(piece, d_row, d_chan)
    bands = [
        jnp.concatenate([parts[d_row, 1], parts[d_row, 0], parts[d_row, -1]], axis=-1)
        for d_row in (1, 0, -1)
    ]
    return jnp.concatenate(bands, axis=-2)


def rows_halo_pair(first, second, width):
    count = lax.axis_size("rows")
    forward = [(i, i + 1) for i in range(count - 1)]
    backward = [(target, source) for source, target in forward]

    def packed(rows):
        a, b = first[..., rows, :], second[..., rows, :]
        return jnp.concatenate([a.reshape(-1), b.reshape(-1)]), a.shape, b.shape

    def unpacked(flat, a_shape, b_shape):
        split = math.prod(a_shape)
        return flat[:split].reshape(a_shape), flat[split:].reshape(b_shape)

    low, a_shape, b_shape = packed(slice(-width, None))
    high, _, _ = packed(slice(0, width))
    low_a, low_b = unpacked(lax.ppermute(low, "rows", forward), a_shape, b_shape)
    high_a, high_b = unpacked(lax.ppermute(high, "rows", backward), a_shape, b_shape)
    return (
        jnp.concatenate([low_a, first, high_a], axis=-2),
        jnp.concatenate([low_b, second, high_b], axis=-2),
    )


def advance(padded, speed_x, speed_y, band):
    center = padded[1:-1, 1:-1]
    back_x = center - padded[:-2, 1:-1]
    ahead_x = padded[2:, 1:-1] - center
    back_y = center - padded[1:-1, :-2]
    ahead_y = padded[1:-1, 2:] - center
    transport = jnp.maximum(speed_x, 0.0) * back_x + jnp.minimum(speed_x, 0.0) * ahead_x
    transport = transport + jnp.maximum(speed_y, 0.0) * back_y + jnp.minimum(speed_y, 0.0) * ahead_y
    return center - time_step * band * transport


def on_device(
    hidden,
    front,
    spectral_weight,
    skip_gain,
    skip_bias,
    project_weight,
    project_bias,
    ice_mask,
    front_flags,
):
    halo = LS_STEPS
    local_chan, row_count, columns = hidden.shape
    row_devices = lax.axis_size("rows")
    chan_devices = lax.axis_size("chan")
    local_ymodes = spectral_weight.shape[1]
    all_rows = row_count * row_devices
    all_xmodes = spectral_weight.shape[2] * chan_devices
    all_ymodes = local_ymodes * row_devices
    tile_cols = columns // chan_devices
    win_rows = row_count + 2 * halo
    norm_scale = 1.0 / math.sqrt(all_rows * columns * all_xmodes * all_ymodes)

    fields = jnp.stack(
        [front, front_flags.astype(jnp.float32), ice_mask.astype(jnp.float32)]
    )
    hidden_win, fields = rows_halo_pair(hidden, fields, halo)
    fields = with_halo(fields, (("chan", 2),), halo)
    fields, hidden_win = lax.optimization_barrier((fields, hidden_win))

    table = base_table(all_ymodes, columns)
    half = all_xmodes // 2
    if all_rows == columns and all_ymodes > half:
        x_table = table
    else:
        x_table = base_table(half + 1, all_rows)
    x_modes = x_table.shape[0] // 2

    spec_y = jnp.einsum("cxy,ky->ckx", hidden, table, precision=highest)
    spec_y = spec_y.reshape(local_chan, 2, all_ymodes, row_count)
    weights = lax.all_to_all(spectral_weight, "chan", split_axis=3, concat_axis=2, tiled=True)
    weights, spec_y = lax.optimization_barrier((weights, spec_y))
    by_freq = lax.all_to_all(spec_y, "rows", split_axis=2, concat_axis=3, tiled=True)
    parts = jnp.einsum("caqx,kx->caqk", by_freq, x_table, precision=highest)
    cos_part = parts[..., :x_modes]
    sin_part = parts[..., x_modes:]
    real_in = unfold_modes(
        cos_part[:, 0] - sin_part[:, 1], cos_part[:, 0] + sin_part[:, 1], half
    )
    imag_in = unfold_modes(
        cos_part[:, 1] + sin_part[:, 0], cos_part[:, 1] - sin_part[:, 0], half
    )
    spectra = jnp.stack([real_in, imag_in], axis=2)

    real_in = spectra[:, :, 0]
    imag_in = spectra[:, :, 1]
    real_out = jnp.einsum(
        "qpio,iqp->oqp", weights[0], real_in, precision=highest
    ) - jnp.einsum("qpio,iqp->oqp", weights[1], imag_in, precision=highest)
    imag_out = jnp.einsum(
        "qpio,iqp->oqp", weights[0], imag_in, precision=highest
    ) + jnp.einsum("qpio,iqp->oqp", weights[1], real_in, precision=highest)
    partial_mixed = jnp.stack([real_out, imag_out], axis=2).reshape(
        (chan_devices, local_chan) + real_out.shape[1:2] + (2,) + real_out.shape[2:]
    )
    mixed = jnp.sum(
        lax.all_to_all(partial_mixed, "chan", split_axis=0, concat_axis=0, tiled=True), axis=0
    )

    real_pos, real_neg = fold_modes(mixed[:, :, 0], half)
    imag_pos, imag_neg = fold_modes(mixed[:, :, 1], half)
    pad = [(0, 0), (0, 0), (0, x_modes - half - 1)]
    coef_real = jnp.concatenate(
        [jnp.pad(real_pos + real_neg, pad), jnp.pad(imag_pos - imag_neg, pad)], axis=-1
    )
    coef_imag = jnp.concatenate(
        [jnp.pad(imag_pos + imag_neg, pad), jnp.pad(real_neg - real_pos, pad)], axis=-1
    )
    coef = jnp.stack([coef_real, coef_imag], axis=1)
    inverted = jnp.einsum("otqk,kx->otqx", coef, x_table, precision=highest)
    inverted = windows(inverted, row_devices, row_count, halo)
    inverted = lax.all_to_all(inverted, "rows", split_axis=3, concat_axis=2, tiled=True)
    y_weights = jnp.where(jnp.arange(all_ymodes) == 0, 1.0, 2.0).astype(jnp.float32) * norm_scale
    inverted = inverted.reshape(local_chan, 2, all_ymodes, win_rows) * y_weights[:, None]
    inverted = inverted.reshape(local_chan, 2 * all_ymodes, win_rows)

    spectral = jnp.einsum("ckx,ky->cxy", inverted, table, precision=highest)
    activated = jax.nn.gelu(
        spectral + skip_gain[:, None, None] * hidden_win + skip_bias[:, None, None],
        approximate=False,
    )
    partial_speed = jnp.einsum("jc,cxy->jxy", project_weight, activated, precision=highest)
    sent = windows(partial_speed, chan_devices, tile_cols, halo)
    received = lax.all_to_all(sent, "chan", split_axis=2, concat_axis=2, tiled=True)
    speed = jnp.sum(received, axis=2) + project_bias[:, None, None]
    speed = speed * fields[2][None]
    velocity = speed[:, halo : halo + row_count, halo : halo + tile_cols]

    level = fields[0]
    band = fields[1]
    for level_step in range(LS_STEPS):
        inner = level_step + 1
        rows_end = win_rows - inner
        cols_end = tile_cols + 2 * halo - inner
        level = advance(
            level,
            speed[0, inner:rows_end, inner:cols_end],
            speed[1, inner:rows_end, inner:cols_end],
            band[inner:rows_end, inner:cols_end],
        )
    return (velocity, level)


def solution(mesh):
    return jax.shard_map(
        on_device,
        mesh=mesh,
        in_specs=(
            P("chan", "rows", None),
            P("rows", "chan"),
            P(None, "rows", "chan", None, None),
            P("chan"),
            P("chan"),
            P(None, "chan"),
            P(),
            P("rows", "chan"),
            P("rows", "chan"),
        ),
        out_specs=(P(None, "rows", "chan"), P("rows", "chan")),
        check_vma=False,
    )
```

```python
import math

import jax
import jax.numpy as jnp
from jax import lax
from jax.sharding import PartitionSpec as P

LS_STEPS = 4


time_step = 0.25
highest = lax.Precision.HIGHEST
high = lax.Precision.HIGH


def with_halo(block, sides, width):
    for axis, dim in sides:
        count = lax.axis_size(axis)
        forward = [(i, i + 1) for i in range(count - 1)]
        backward = [(target, source) for source, target in forward]
        low = lax.ppermute(
            lax.slice_in_dim(block, block.shape[dim] - width, None, axis=dim), axis, forward
        )
        high = lax.ppermute(lax.slice_in_dim(block, 0, width, axis=dim), axis, backward)
        block = jnp.concatenate([low, block, high], axis=dim)
    return block


def angles(freqs, places, length):
    product = freqs[:, None] * places[None, :] % length
    return 2.0 * math.pi / length * product.astype(jnp.float32)


def base_table(modes, length):
    phase = angles(jnp.arange(modes, dtype=jnp.int32), jnp.arange(length, dtype=jnp.int32), length)
    return jnp.concatenate([jnp.cos(phase), -jnp.sin(phase)])


def fold_modes(vec, half):
    pos = jnp.pad(vec[..., :half], [(0, 0)] * (vec.ndim - 1) + [(0, 1)])
    neg = jnp.pad(jnp.flip(vec[..., half:], -1), [(0, 0)] * (vec.ndim - 1) + [(1, 0)])
    return pos, neg


def unfold_modes(plus, minus, half):
    return jnp.concatenate([plus[..., :half], jnp.flip(minus[..., 1 : half + 1], -1)], axis=-1)


def windows(block, count, size, halo):
    padded = jnp.pad(block, [(0, 0)] * (block.ndim - 1) + [(halo, size)])
    lead = block.shape[:-1]
    main = padded[..., : count * size].reshape(lead + (count, size))
    tail = padded[..., size : size + count * size].reshape(lead + (count, size))
    return jnp.concatenate([main, tail[..., : 2 * halo]], axis=-1)


def halo_2d(block, width):
    n_rows = lax.axis_size("rows")
    n_chan = lax.axis_size("chan")

    def shifted(piece, d_row, d_chan):
        pairs = [
            (r * n_chan + c, (r + d_row) * n_chan + c + d_chan)
            for r in range(n_rows)
            for c in range(n_chan)
            if 0 <= r + d_row < n_rows and 0 <= c + d_chan < n_chan
        ]
        return lax.ppermute(piece, ("rows", "chan"), pairs)

    lo, hi = slice(-width, None), slice(0, width)
    every = slice(None)
    parts = {}
    for d_row, rows in ((1, lo), (0, every), (-1, hi)):
        for d_chan, cols in ((1, lo), (0, every), (-1, hi)):
            piece = block[..., rows, cols]
            parts[d_row, d_chan] = piece if d_row == d_chan == 0 else shifted(piece, d_row, d_chan)
    bands = [
        jnp.concatenate([parts[d_row, 1], parts[d_row, 0], parts[d_row, -1]], axis=-1)
        for d_row in (1, 0, -1)
    ]
    return jnp.concatenate(bands, axis=-2)


def rows_halo_pair(first, second, width):
    count = lax.axis_size("rows")
    forward = [(i, i + 1) for i in range(count - 1)]
    backward = [(target, source) for source, target in forward]

    def packed(rows):
        a, b = first[..., rows, :], second[..., rows, :]
        return jnp.concatenate([a.reshape(-1), b.reshape(-1)]), a.shape, b.shape

    def unpacked(flat, a_shape, b_shape):
        split = math.prod(a_shape)
        return flat[:split].reshape(a_shape), flat[split:].reshape(b_shape)

    low, a_shape, b_shape = packed(slice(-width, None))
    high, _, _ = packed(slice(0, width))
    low_a, low_b = unpacked(lax.ppermute(low, "rows", forward), a_shape, b_shape)
    high_a, high_b = unpacked(lax.ppermute(high, "rows", backward), a_shape, b_shape)
    return (
        jnp.concatenate([low_a, first, high_a], axis=-2),
        jnp.concatenate([low_b, second, high_b], axis=-2),
    )


def advance(padded, speed_x, speed_y, band):
    center = padded[1:-1, 1:-1]
    back_x = center - padded[:-2, 1:-1]
    ahead_x = padded[2:, 1:-1] - center
    back_y = center - padded[1:-1, :-2]
    ahead_y = padded[1:-1, 2:] - center
    transport = jnp.maximum(speed_x, 0.0) * back_x + jnp.minimum(speed_x, 0.0) * ahead_x
    transport = transport + jnp.maximum(speed_y, 0.0) * back_y + jnp.minimum(speed_y, 0.0) * ahead_y
    return center - time_step * band * transport


def on_device(
    hidden,
    front,
    spectral_weight,
    skip_gain,
    skip_bias,
    project_weight,
    project_bias,
    ice_mask,
    front_flags,
):
    halo = LS_STEPS
    local_chan, row_count, columns = hidden.shape
    row_devices = lax.axis_size("rows")
    chan_devices = lax.axis_size("chan")
    local_ymodes = spectral_weight.shape[1]
    all_rows = row_count * row_devices
    all_xmodes = spectral_weight.shape[2] * chan_devices
    all_ymodes = local_ymodes * row_devices
    tile_cols = columns // chan_devices
    win_rows = row_count + 2 * halo
    norm_scale = 1.0 / math.sqrt(all_rows * columns * all_xmodes * all_ymodes)

    fields = jnp.stack(
        [front, front_flags.astype(jnp.float32), ice_mask.astype(jnp.float32)]
    )
    hidden_win, fields = rows_halo_pair(hidden, fields, halo)
    fields = with_halo(fields, (("chan", 2),), halo)
    fields, hidden_win = lax.optimization_barrier((fields, hidden_win))

    table = base_table(all_ymodes, columns)
    half = all_xmodes // 2
    if all_rows == columns and all_ymodes > half:
        x_table = table
    else:
        x_table = base_table(half + 1, all_rows)
    x_modes = x_table.shape[0] // 2

    spec_y = jnp.einsum("cxy,ky->ckx", hidden, table, precision=high)
    spec_y = spec_y.reshape(local_chan, 2, all_ymodes, row_count)
    by_freq = lax.all_to_all(spec_y, "rows", split_axis=2, concat_axis=3, tiled=True)
    parts = jnp.einsum("caqx,kx->caqk", by_freq, x_table, precision=high)
    cos_part = parts[..., :x_modes]
    sin_part = parts[..., x_modes:]
    real_in = unfold_modes(
        cos_part[:, 0] - sin_part[:, 1], cos_part[:, 0] + sin_part[:, 1], half
    )
    imag_in = unfold_modes(
        cos_part[:, 1] + sin_part[:, 0], cos_part[:, 1] - sin_part[:, 0], half
    )
    spectra = jnp.stack([real_in, imag_in], axis=2)

    gathered = lax.all_to_all(spectra, "chan", split_axis=3, concat_axis=0, tiled=True)
    real_in = gathered[:, :, 0]
    imag_in = gathered[:, :, 1]
    real_out = jnp.einsum(
        "qpio,iqp->oqp", spectral_weight[0], real_in, precision=highest
    ) - jnp.einsum("qpio,iqp->oqp", spectral_weight[1], imag_in, precision=highest)
    imag_out = jnp.einsum(
        "qpio,iqp->oqp", spectral_weight[0], imag_in, precision=highest
    ) + jnp.einsum("qpio,iqp->oqp", spectral_weight[1], real_in, precision=highest)
    mixed = lax.all_to_all(
        jnp.stack([real_out, imag_out], axis=2), "chan", split_axis=0, concat_axis=3, tiled=True
    )

    real_pos, real_neg = fold_modes(mixed[:, :, 0], half)
    imag_pos, imag_neg = fold_modes(mixed[:, :, 1], half)
    pad = [(0, 0), (0, 0), (0, x_modes - half - 1)]
    coef_real = jnp.concatenate(
        [jnp.pad(real_pos + real_neg, pad), jnp.pad(imag_pos - imag_neg, pad)], axis=-1
    )
    coef_imag = jnp.concatenate(
        [jnp.pad(imag_pos + imag_neg, pad), jnp.pad(real_neg - real_pos, pad)], axis=-1
    )
    coef = jnp.stack([coef_real, coef_imag], axis=1)
    inverted = jnp.einsum("otqk,kx->otqx", coef, x_table, precision=high)
    inverted = windows(inverted, row_devices, row_count, halo)
    inverted = lax.all_to_all(inverted, "rows", split_axis=3, concat_axis=2, tiled=True)
    y_weights = jnp.where(jnp.arange(all_ymodes) == 0, 1.0, 2.0).astype(jnp.float32) * norm_scale
    inverted = inverted.reshape(local_chan, 2, all_ymodes, win_rows) * y_weights[:, None]
    inverted = inverted.reshape(local_chan, 2 * all_ymodes, win_rows)

    spectral = jnp.einsum("ckx,ky->cxy", inverted, table, precision=high)
    activated = jax.nn.gelu(
        spectral + skip_gain[:, None, None] * hidden_win + skip_bias[:, None, None],
        approximate=False,
    )
    partial_speed = jnp.sum(project_weight[:, :, None, None] * activated[None], axis=1)
    sent = windows(partial_speed, chan_devices, tile_cols, halo)
    received = lax.all_to_all(sent, "chan", split_axis=2, concat_axis=2, tiled=True)
    speed = jnp.sum(received, axis=2) + project_bias[:, None, None]
    speed = speed * fields[2][None]
    velocity = speed[:, halo : halo + row_count, halo : halo + tile_cols]

    level = fields[0]
    band = fields[1]
    for level_step in range(LS_STEPS):
        inner = level_step + 1
        rows_end = win_rows - inner
        cols_end = tile_cols + 2 * halo - inner
        level = advance(
            level,
            speed[0, inner:rows_end, inner:cols_end],
            speed[1, inner:rows_end, inner:cols_end],
            band[inner:rows_end, inner:cols_end],
        )
    return (velocity, level)


def solution(mesh):
    return jax.shard_map(
        on_device,
        mesh=mesh,
        in_specs=(
            P("chan", "rows", None),
            P("rows", "chan"),
            P(None, "rows", "chan", None, None),
            P("chan"),
            P("chan"),
            P(None, "chan"),
            P(),
            P("rows", "chan"),
            P("rows", "chan"),
        ),
        out_specs=(P(None, "rows", "chan"), P("rows", "chan")),
        check_vma=False,
    )
```

```python
import math

import jax
import jax.numpy as jnp
from jax import lax
from jax.sharding import PartitionSpec as P

LS_STEPS = 4


time_step = 0.25
highest = lax.Precision.HIGHEST
high = lax.Precision.HIGH


def with_halo(block, sides, width):
    for axis, dim in sides:
        count = lax.axis_size(axis)
        forward = [(i, i + 1) for i in range(count - 1)]
        backward = [(target, source) for source, target in forward]
        low = lax.ppermute(
            lax.slice_in_dim(block, block.shape[dim] - width, None, axis=dim), axis, forward
        )
        high = lax.ppermute(lax.slice_in_dim(block, 0, width, axis=dim), axis, backward)
        block = jnp.concatenate([low, block, high], axis=dim)
    return block


def angles(freqs, places, length):
    product = freqs[:, None] * places[None, :] % length
    return 2.0 * math.pi / length * product.astype(jnp.float32)


def base_table(modes, length):
    phase = angles(jnp.arange(modes, dtype=jnp.int32), jnp.arange(length, dtype=jnp.int32), length)
    return jnp.concatenate([jnp.cos(phase), -jnp.sin(phase)])


def fold_modes(vec, half):
    pos = jnp.pad(vec[..., :half], [(0, 0)] * (vec.ndim - 1) + [(0, 1)])
    neg = jnp.pad(jnp.flip(vec[..., half:], -1), [(0, 0)] * (vec.ndim - 1) + [(1, 0)])
    return pos, neg


def unfold_modes(plus, minus, half):
    return jnp.concatenate([plus[..., :half], jnp.flip(minus[..., 1 : half + 1], -1)], axis=-1)


def windows(block, count, size, halo):
    padded = jnp.pad(block, [(0, 0)] * (block.ndim - 1) + [(halo, size)])
    lead = block.shape[:-1]
    main = padded[..., : count * size].reshape(lead + (count, size))
    tail = padded[..., size : size + count * size].reshape(lead + (count, size))
    return jnp.concatenate([main, tail[..., : 2 * halo]], axis=-1)


def halo_2d(block, width):
    n_rows = lax.axis_size("rows")
    n_chan = lax.axis_size("chan")

    def shifted(piece, d_row, d_chan):
        pairs = [
            (r * n_chan + c, (r + d_row) * n_chan + c + d_chan)
            for r in range(n_rows)
            for c in range(n_chan)
            if 0 <= r + d_row < n_rows and 0 <= c + d_chan < n_chan
        ]
        return lax.ppermute(piece, ("rows", "chan"), pairs)

    lo, hi = slice(-width, None), slice(0, width)
    every = slice(None)
    parts = {}
    for d_row, rows in ((1, lo), (0, every), (-1, hi)):
        for d_chan, cols in ((1, lo), (0, every), (-1, hi)):
            piece = block[..., rows, cols]
            parts[d_row, d_chan] = piece if d_row == d_chan == 0 else shifted(piece, d_row, d_chan)
    bands = [
        jnp.concatenate([parts[d_row, 1], parts[d_row, 0], parts[d_row, -1]], axis=-1)
        for d_row in (1, 0, -1)
    ]
    return jnp.concatenate(bands, axis=-2)


def rows_halo_pair(first, second, width):
    count = lax.axis_size("rows")
    forward = [(i, i + 1) for i in range(count - 1)]
    backward = [(target, source) for source, target in forward]

    def packed(rows):
        a, b = first[..., rows, :], second[..., rows, :]
        return jnp.concatenate([a.reshape(-1), b.reshape(-1)]), a.shape, b.shape

    def unpacked(flat, a_shape, b_shape):
        split = math.prod(a_shape)
        return flat[:split].reshape(a_shape), flat[split:].reshape(b_shape)

    low, a_shape, b_shape = packed(slice(-width, None))
    high, _, _ = packed(slice(0, width))
    low_a, low_b = unpacked(lax.ppermute(low, "rows", forward), a_shape, b_shape)
    high_a, high_b = unpacked(lax.ppermute(high, "rows", backward), a_shape, b_shape)
    return (
        jnp.concatenate([low_a, first, high_a], axis=-2),
        jnp.concatenate([low_b, second, high_b], axis=-2),
    )


def advance(padded, speed_x, speed_y, band):
    center = padded[1:-1, 1:-1]
    back_x = center - padded[:-2, 1:-1]
    ahead_x = padded[2:, 1:-1] - center
    back_y = center - padded[1:-1, :-2]
    ahead_y = padded[1:-1, 2:] - center
    transport = jnp.maximum(speed_x, 0.0) * back_x + jnp.minimum(speed_x, 0.0) * ahead_x
    transport = transport + jnp.maximum(speed_y, 0.0) * back_y + jnp.minimum(speed_y, 0.0) * ahead_y
    return center - time_step * band * transport


def on_device(
    hidden,
    front,
    spectral_weight,
    skip_gain,
    skip_bias,
    project_weight,
    project_bias,
    ice_mask,
    front_flags,
):
    halo = LS_STEPS
    local_chan, row_count, columns = hidden.shape
    row_devices = lax.axis_size("rows")
    chan_devices = lax.axis_size("chan")
    local_ymodes = spectral_weight.shape[1]
    all_rows = row_count * row_devices
    all_xmodes = spectral_weight.shape[2] * chan_devices
    all_ymodes = local_ymodes * row_devices
    tile_cols = columns // chan_devices
    win_rows = row_count + 2 * halo
    norm_scale = 1.0 / math.sqrt(all_rows * columns * all_xmodes * all_ymodes)

    fields = jnp.stack(
        [front, front_flags.astype(jnp.float32), ice_mask.astype(jnp.float32)]
    )
    hidden_win, fields = rows_halo_pair(hidden, fields, halo)
    fields = with_halo(fields, (("chan", 2),), halo)
    fields, hidden_win = lax.optimization_barrier((fields, hidden_win))

    table = base_table(all_ymodes, columns)
    half = all_xmodes // 2
    if all_rows == columns and all_ymodes > half:
        x_table = table
    else:
        x_table = base_table(half + 1, all_rows)
    x_modes = x_table.shape[0] // 2

    spec_y = jnp.einsum("cxy,ky->ckx", hidden, table, precision=high)
    spec_y = spec_y.reshape(local_chan, 2, all_ymodes, row_count)
    by_freq = lax.all_to_all(spec_y, "rows", split_axis=2, concat_axis=3, tiled=True)
    parts = jnp.einsum("caqx,kx->caqk", by_freq, x_table, precision=high)
    cos_part = parts[..., :x_modes]
    sin_part = parts[..., x_modes:]
    real_in = unfold_modes(
        cos_part[:, 0] - sin_part[:, 1], cos_part[:, 0] + sin_part[:, 1], half
    )
    imag_in = unfold_modes(
        cos_part[:, 1] + sin_part[:, 0], cos_part[:, 1] - sin_part[:, 0], half
    )
    spectra = jnp.stack([real_in, imag_in], axis=2)

    gathered = lax.all_to_all(spectra, "chan", split_axis=3, concat_axis=0, tiled=True)
    real_in = gathered[:, :, 0]
    imag_in = gathered[:, :, 1]
    real_out = jnp.einsum(
        "qpio,iqp->oqp", spectral_weight[0], real_in, precision=highest
    ) - jnp.einsum("qpio,iqp->oqp", spectral_weight[1], imag_in, precision=highest)
    imag_out = jnp.einsum(
        "qpio,iqp->oqp", spectral_weight[0], imag_in, precision=highest
    ) + jnp.einsum("qpio,iqp->oqp", spectral_weight[1], real_in, precision=highest)
    mixed = lax.all_to_all(
        jnp.stack([real_out, imag_out], axis=2), "chan", split_axis=0, concat_axis=3, tiled=True
    )

    real_pos, real_neg = fold_modes(mixed[:, :, 0], half)
    imag_pos, imag_neg = fold_modes(mixed[:, :, 1], half)
    pad = [(0, 0), (0, 0), (0, x_modes - half - 1)]
    coef_real = jnp.concatenate(
        [jnp.pad(real_pos + real_neg, pad), jnp.pad(imag_pos - imag_neg, pad)], axis=-1
    )
    coef_imag = jnp.concatenate(
        [jnp.pad(imag_pos + imag_neg, pad), jnp.pad(real_neg - real_pos, pad)], axis=-1
    )
    coef = jnp.stack([coef_real, coef_imag], axis=1)
    inverted = jnp.einsum("otqk,kx->otqx", coef, x_table, precision=high)
    inverted = windows(inverted, row_devices, row_count, halo)
    inverted = lax.all_to_all(inverted, "rows", split_axis=3, concat_axis=2, tiled=True)
    y_weights = jnp.where(jnp.arange(all_ymodes) == 0, 1.0, 2.0).astype(jnp.float32) * norm_scale
    inverted = inverted.reshape(local_chan, 2, all_ymodes, win_rows) * y_weights[:, None]
    inverted = inverted.reshape(local_chan, 2 * all_ymodes, win_rows)

    spectral = jnp.einsum("ckx,ky->cxy", inverted, table, precision=high)
    activated = jax.nn.gelu(
        spectral + skip_gain[:, None, None] * hidden_win + skip_bias[:, None, None],
        approximate=False,
    )
    partial_speed = jnp.sum(project_weight[:, :, None, None] * activated[None], axis=1)
    sent = windows(partial_speed, chan_devices, tile_cols, halo)
    sent = jnp.moveaxis(sent, 2, 0)
    chunk_shape = sent.shape[1:]
    chunk = math.prod(chunk_shape)
    lanes = 128
    flat_len = -(-chunk // lanes) * lanes
    flat = jnp.pad(sent.reshape(chan_devices, chunk), ((0, 0), (0, flat_len - chunk)))
    flat = flat.reshape(chan_devices, flat_len // lanes, lanes)
    received = lax.all_to_all(flat, "chan", split_axis=0, concat_axis=0, tiled=True)
    speed = jnp.sum(received, axis=0).reshape(-1)[:chunk].reshape(chunk_shape)
    speed = speed + project_bias[:, None, None]
    speed = speed * fields[2][None]
    velocity = speed[:, halo : halo + row_count, halo : halo + tile_cols]

    level = fields[0]
    band = fields[1]
    for level_step in range(LS_STEPS):
        inner = level_step + 1
        rows_end = win_rows - inner
        cols_end = tile_cols + 2 * halo - inner
        level = advance(
            level,
            speed[0, inner:rows_end, inner:cols_end],
            speed[1, inner:rows_end, inner:cols_end],
            band[inner:rows_end, inner:cols_end],
        )
    return (velocity, level)


def solution(mesh):
    return jax.shard_map(
        on_device,
        mesh=mesh,
        in_specs=(
            P("chan", "rows", None),
            P("rows", "chan"),
            P(None, "rows", "chan", None, None),
            P("chan"),
            P("chan"),
            P(None, "chan"),
            P(),
            P("rows", "chan"),
            P("rows", "chan"),
        ),
        out_specs=(P(None, "rows", "chan"), P("rows", "chan")),
        check_vma=False,
    )
```

```python
import math

import jax
import jax.numpy as jnp
from jax import lax
from jax.sharding import PartitionSpec as P

LS_STEPS = 4


time_step = 0.25
highest = lax.Precision.HIGHEST
high = lax.Precision.HIGH


def with_halo(block, sides, width):
    for axis, dim in sides:
        count = lax.axis_size(axis)
        forward = [(i, i + 1) for i in range(count - 1)]
        backward = [(target, source) for source, target in forward]
        low = lax.ppermute(
            lax.slice_in_dim(block, block.shape[dim] - width, None, axis=dim), axis, forward
        )
        high = lax.ppermute(lax.slice_in_dim(block, 0, width, axis=dim), axis, backward)
        block = jnp.concatenate([low, block, high], axis=dim)
    return block


def angles(freqs, places, length):
    product = freqs[:, None] * places[None, :] % length
    return 2.0 * math.pi / length * product.astype(jnp.float32)


def base_table(modes, length):
    phase = angles(jnp.arange(modes, dtype=jnp.int32), jnp.arange(length, dtype=jnp.int32), length)
    return jnp.concatenate([jnp.cos(phase), -jnp.sin(phase)])


def fold_modes(vec, half):
    pos = jnp.pad(vec[..., :half], [(0, 0)] * (vec.ndim - 1) + [(0, 1)])
    neg = jnp.pad(jnp.flip(vec[..., half:], -1), [(0, 0)] * (vec.ndim - 1) + [(1, 0)])
    return pos, neg


def unfold_modes(plus, minus, half):
    return jnp.concatenate([plus[..., :half], jnp.flip(minus[..., 1 : half + 1], -1)], axis=-1)


def windows(block, count, size, halo):
    padded = jnp.pad(block, [(0, 0)] * (block.ndim - 1) + [(halo, size)])
    lead = block.shape[:-1]
    main = padded[..., : count * size].reshape(lead + (count, size))
    tail = padded[..., size : size + count * size].reshape(lead + (count, size))
    return jnp.concatenate([main, tail[..., : 2 * halo]], axis=-1)


def halo_2d(block, width):
    n_rows = lax.axis_size("rows")
    n_chan = lax.axis_size("chan")

    def shifted(piece, d_row, d_chan):
        pairs = [
            (r * n_chan + c, (r + d_row) * n_chan + c + d_chan)
            for r in range(n_rows)
            for c in range(n_chan)
            if 0 <= r + d_row < n_rows and 0 <= c + d_chan < n_chan
        ]
        return lax.ppermute(piece, ("rows", "chan"), pairs)

    lo, hi = slice(-width, None), slice(0, width)
    every = slice(None)
    parts = {}
    for d_row, rows in ((1, lo), (0, every), (-1, hi)):
        for d_chan, cols in ((1, lo), (0, every), (-1, hi)):
            piece = block[..., rows, cols]
            parts[d_row, d_chan] = piece if d_row == d_chan == 0 else shifted(piece, d_row, d_chan)
    bands = [
        jnp.concatenate([parts[d_row, 1], parts[d_row, 0], parts[d_row, -1]], axis=-1)
        for d_row in (1, 0, -1)
    ]
    return jnp.concatenate(bands, axis=-2)


def rows_halo_pair(first, second, width):
    count = lax.axis_size("rows")
    forward = [(i, i + 1) for i in range(count - 1)]
    backward = [(target, source) for source, target in forward]

    def packed(rows):
        a, b = first[..., rows, :], second[..., rows, :]
        return jnp.concatenate([a.reshape(-1), b.reshape(-1)]), a.shape, b.shape

    def unpacked(flat, a_shape, b_shape):
        split = math.prod(a_shape)
        return flat[:split].reshape(a_shape), flat[split:].reshape(b_shape)

    low, a_shape, b_shape = packed(slice(-width, None))
    high, _, _ = packed(slice(0, width))
    low_a, low_b = unpacked(lax.ppermute(low, "rows", forward), a_shape, b_shape)
    high_a, high_b = unpacked(lax.ppermute(high, "rows", backward), a_shape, b_shape)
    return (
        jnp.concatenate([low_a, first, high_a], axis=-2),
        jnp.concatenate([low_b, second, high_b], axis=-2),
    )


def advance(padded, speed_x, speed_y, band):
    center = padded[1:-1, 1:-1]
    back_x = center - padded[:-2, 1:-1]
    ahead_x = padded[2:, 1:-1] - center
    back_y = center - padded[1:-1, :-2]
    ahead_y = padded[1:-1, 2:] - center
    transport = jnp.maximum(speed_x, 0.0) * back_x + jnp.minimum(speed_x, 0.0) * ahead_x
    transport = transport + jnp.maximum(speed_y, 0.0) * back_y + jnp.minimum(speed_y, 0.0) * ahead_y
    return center - time_step * band * transport


def on_device(
    hidden,
    front,
    spectral_weight,
    skip_gain,
    skip_bias,
    project_weight,
    project_bias,
    ice_mask,
    front_flags,
):
    halo = LS_STEPS
    local_chan, row_count, columns = hidden.shape
    row_devices = lax.axis_size("rows")
    chan_devices = lax.axis_size("chan")
    local_ymodes = spectral_weight.shape[1]
    all_rows = row_count * row_devices
    all_xmodes = spectral_weight.shape[2] * chan_devices
    all_ymodes = local_ymodes * row_devices
    tile_cols = columns // chan_devices
    win_rows = row_count + 2 * halo
    norm_scale = 1.0 / math.sqrt(all_rows * columns * all_xmodes * all_ymodes)

    fields = jnp.stack(
        [front, front_flags.astype(jnp.float32), ice_mask.astype(jnp.float32)]
    )
    hidden_win, fields = rows_halo_pair(hidden, fields, halo)
    fields = with_halo(fields, (("chan", 2),), halo)
    fields, hidden_win = lax.optimization_barrier((fields, hidden_win))

    table = base_table(all_ymodes, columns)
    half = all_xmodes // 2
    if all_rows == columns and all_ymodes > half:
        x_table = table
    else:
        x_table = base_table(half + 1, all_rows)
    x_modes = x_table.shape[0] // 2

    spec_y = jnp.einsum("cxy,ky->ckx", hidden, table, precision=high)
    spec_y = spec_y.reshape(local_chan, 2, row_devices, local_ymodes, row_count)
    by_freq = lax.all_to_all(spec_y, "rows", split_axis=2, concat_axis=0, tiled=False)
    blocked_table = x_table.reshape(x_table.shape[0], row_devices, row_count)
    parts = jnp.einsum("scaqx,ksx->caqk", by_freq, blocked_table, precision=high)
    cos_part = parts[..., :x_modes]
    sin_part = parts[..., x_modes:]
    real_in = unfold_modes(
        cos_part[:, 0] - sin_part[:, 1], cos_part[:, 0] + sin_part[:, 1], half
    )
    imag_in = unfold_modes(
        cos_part[:, 1] + sin_part[:, 0], cos_part[:, 1] - sin_part[:, 0], half
    )
    spectra = jnp.stack([real_in, imag_in], axis=2)

    gathered = lax.all_to_all(spectra, "chan", split_axis=3, concat_axis=0, tiled=True)
    real_in = gathered[:, :, 0]
    imag_in = gathered[:, :, 1]
    real_out = jnp.einsum(
        "qpio,iqp->oqp", spectral_weight[0], real_in, precision=highest
    ) - jnp.einsum("qpio,iqp->oqp", spectral_weight[1], imag_in, precision=highest)
    imag_out = jnp.einsum(
        "qpio,iqp->oqp", spectral_weight[0], imag_in, precision=highest
    ) + jnp.einsum("qpio,iqp->oqp", spectral_weight[1], real_in, precision=highest)
    mixed = lax.all_to_all(
        jnp.stack([real_out, imag_out], axis=2), "chan", split_axis=0, concat_axis=3, tiled=True
    )

    real_pos, real_neg = fold_modes(mixed[:, :, 0], half)
    imag_pos, imag_neg = fold_modes(mixed[:, :, 1], half)
    pad = [(0, 0), (0, 0), (0, x_modes - half - 1)]
    coef_real = jnp.concatenate(
        [jnp.pad(real_pos + real_neg, pad), jnp.pad(imag_pos - imag_neg, pad)], axis=-1
    )
    coef_imag = jnp.concatenate(
        [jnp.pad(imag_pos + imag_neg, pad), jnp.pad(real_neg - real_pos, pad)], axis=-1
    )
    coef = jnp.stack([coef_real, coef_imag], axis=1)
    inverted = jnp.einsum("otqk,kx->otqx", coef, x_table, precision=high)
    inverted = windows(inverted, row_devices, row_count, halo)
    inverted = lax.all_to_all(inverted, "rows", split_axis=3, concat_axis=2, tiled=True)
    y_weights = jnp.where(jnp.arange(all_ymodes) == 0, 1.0, 2.0).astype(jnp.float32) * norm_scale
    inverted = inverted.reshape(local_chan, 2, all_ymodes, win_rows) * y_weights[:, None]
    inverted = inverted.reshape(local_chan, 2 * all_ymodes, win_rows)

    spectral = jnp.einsum("ckx,ky->cxy", inverted, table, precision=high)
    activated = jax.nn.gelu(
        spectral + skip_gain[:, None, None] * hidden_win + skip_bias[:, None, None],
        approximate=False,
    )
    partial_speed = jnp.sum(project_weight[:, :, None, None] * activated[None], axis=1)
    sent = windows(partial_speed, chan_devices, tile_cols, halo)
    sent = jnp.moveaxis(sent, 2, 0)
    chunk_shape = sent.shape[1:]
    chunk = math.prod(chunk_shape)
    lanes = 128
    flat_len = -(-chunk // lanes) * lanes
    flat = jnp.pad(sent.reshape(chan_devices, chunk), ((0, 0), (0, flat_len - chunk)))
    flat = flat.reshape(chan_devices, flat_len // lanes, lanes)
    received = lax.all_to_all(flat, "chan", split_axis=0, concat_axis=0, tiled=True)
    speed = jnp.sum(received, axis=0).reshape(-1)[:chunk].reshape(chunk_shape)
    speed = speed + project_bias[:, None, None]
    speed = speed * fields[2][None]
    velocity = speed[:, halo : halo + row_count, halo : halo + tile_cols]

    level = fields[0]
    band = fields[1]
    for level_step in range(LS_STEPS):
        inner = level_step + 1
        rows_end = win_rows - inner
        cols_end = tile_cols + 2 * halo - inner
        level = advance(
            level,
            speed[0, inner:rows_end, inner:cols_end],
            speed[1, inner:rows_end, inner:cols_end],
            band[inner:rows_end, inner:cols_end],
        )
    return (velocity, level)


def solution(mesh):
    return jax.shard_map(
        on_device,
        mesh=mesh,
        in_specs=(
            P("chan", "rows", None),
            P("rows", "chan"),
            P(None, "rows", "chan", None, None),
            P("chan"),
            P("chan"),
            P(None, "chan"),
            P(),
            P("rows", "chan"),
            P("rows", "chan"),
        ),
        out_specs=(P(None, "rows", "chan"), P("rows", "chan")),
        check_vma=False,
    )
```

```python
import math

import jax
import jax.numpy as jnp
from jax import lax
from jax.sharding import PartitionSpec as P

LS_STEPS = 4


time_step = 0.25
highest = lax.Precision.HIGHEST
high = lax.Precision.HIGH


def with_halo(block, sides, width):
    for axis, dim in sides:
        count = lax.axis_size(axis)
        forward = [(i, i + 1) for i in range(count - 1)]
        backward = [(target, source) for source, target in forward]
        low = lax.ppermute(
            lax.slice_in_dim(block, block.shape[dim] - width, None, axis=dim), axis, forward
        )
        high = lax.ppermute(lax.slice_in_dim(block, 0, width, axis=dim), axis, backward)
        block = jnp.concatenate([low, block, high], axis=dim)
    return block


def angles(freqs, places, length):
    product = freqs[:, None] * places[None, :] % length
    return 2.0 * math.pi / length * product.astype(jnp.float32)


def base_table(modes, length):
    phase = angles(jnp.arange(modes, dtype=jnp.int32), jnp.arange(length, dtype=jnp.int32), length)
    return jnp.concatenate([jnp.cos(phase), -jnp.sin(phase)])


def fold_modes(vec, half):
    pos = jnp.pad(vec[..., :half], [(0, 0)] * (vec.ndim - 1) + [(0, 1)])
    neg = jnp.pad(jnp.flip(vec[..., half:], -1), [(0, 0)] * (vec.ndim - 1) + [(1, 0)])
    return pos, neg


def unfold_modes(plus, minus, half):
    return jnp.concatenate([plus[..., :half], jnp.flip(minus[..., 1 : half + 1], -1)], axis=-1)


def windows(block, count, size, halo):
    padded = jnp.pad(block, [(0, 0)] * (block.ndim - 1) + [(halo, size)])
    lead = block.shape[:-1]
    main = padded[..., : count * size].reshape(lead + (count, size))
    tail = padded[..., size : size + count * size].reshape(lead + (count, size))
    return jnp.concatenate([main, tail[..., : 2 * halo]], axis=-1)


def halo_2d(block, width):
    n_rows = lax.axis_size("rows")
    n_chan = lax.axis_size("chan")

    def shifted(piece, d_row, d_chan):
        pairs = [
            (r * n_chan + c, (r + d_row) * n_chan + c + d_chan)
            for r in range(n_rows)
            for c in range(n_chan)
            if 0 <= r + d_row < n_rows and 0 <= c + d_chan < n_chan
        ]
        return lax.ppermute(piece, ("rows", "chan"), pairs)

    lo, hi = slice(-width, None), slice(0, width)
    every = slice(None)
    parts = {}
    for d_row, rows in ((1, lo), (0, every), (-1, hi)):
        for d_chan, cols in ((1, lo), (0, every), (-1, hi)):
            piece = block[..., rows, cols]
            parts[d_row, d_chan] = piece if d_row == d_chan == 0 else shifted(piece, d_row, d_chan)
    bands = [
        jnp.concatenate([parts[d_row, 1], parts[d_row, 0], parts[d_row, -1]], axis=-1)
        for d_row in (1, 0, -1)
    ]
    return jnp.concatenate(bands, axis=-2)


def rows_halo_pair(first, second, width):
    count = lax.axis_size("rows")
    forward = [(i, i + 1) for i in range(count - 1)]
    backward = [(target, source) for source, target in forward]

    def packed(rows):
        a, b = first[..., rows, :], second[..., rows, :]
        return jnp.concatenate([a.reshape(-1), b.reshape(-1)]), a.shape, b.shape

    def unpacked(flat, a_shape, b_shape):
        split = math.prod(a_shape)
        return flat[:split].reshape(a_shape), flat[split:].reshape(b_shape)

    low, a_shape, b_shape = packed(slice(-width, None))
    high, _, _ = packed(slice(0, width))
    low_a, low_b = unpacked(lax.ppermute(low, "rows", forward), a_shape, b_shape)
    high_a, high_b = unpacked(lax.ppermute(high, "rows", backward), a_shape, b_shape)
    return (
        jnp.concatenate([low_a, first, high_a], axis=-2),
        jnp.concatenate([low_b, second, high_b], axis=-2),
    )


def advance(padded, speed_x, speed_y, band):
    center = padded[1:-1, 1:-1]
    back_x = center - padded[:-2, 1:-1]
    ahead_x = padded[2:, 1:-1] - center
    back_y = center - padded[1:-1, :-2]
    ahead_y = padded[1:-1, 2:] - center
    transport = jnp.maximum(speed_x, 0.0) * back_x + jnp.minimum(speed_x, 0.0) * ahead_x
    transport = transport + jnp.maximum(speed_y, 0.0) * back_y + jnp.minimum(speed_y, 0.0) * ahead_y
    return center - time_step * band * transport


def on_device(
    hidden,
    front,
    spectral_weight,
    skip_gain,
    skip_bias,
    project_weight,
    project_bias,
    ice_mask,
    front_flags,
):
    halo = LS_STEPS
    local_chan, row_count, columns = hidden.shape
    row_devices = lax.axis_size("rows")
    chan_devices = lax.axis_size("chan")
    local_ymodes = spectral_weight.shape[1]
    all_rows = row_count * row_devices
    all_xmodes = spectral_weight.shape[2] * chan_devices
    all_ymodes = local_ymodes * row_devices
    tile_cols = columns // chan_devices
    win_rows = row_count + 2 * halo
    norm_scale = 1.0 / math.sqrt(all_rows * columns * all_xmodes * all_ymodes)

    fields = jnp.stack(
        [front, front_flags.astype(jnp.float32), ice_mask.astype(jnp.float32)]
    )

    table = base_table(all_ymodes, columns)
    half = all_xmodes // 2
    if all_rows == columns and all_ymodes > half:
        x_table = table
    else:
        x_table = base_table(half + 1, all_rows)
    x_modes = x_table.shape[0] // 2

    spec_y = jnp.einsum("cxy,ky->ckx", hidden, table, precision=high)
    spec_y = spec_y.reshape(local_chan, 2, all_ymodes, row_count)
    by_freq = lax.all_to_all(spec_y, "rows", split_axis=2, concat_axis=3, tiled=True)
    hidden_late, fields, by_freq = lax.optimization_barrier((hidden, fields, by_freq))
    hidden_win, fields = rows_halo_pair(hidden_late, fields, halo)
    fields = with_halo(fields, (("chan", 2),), halo)
    fields, hidden_win = lax.optimization_barrier((fields, hidden_win))
    parts = jnp.einsum("caqx,kx->caqk", by_freq, x_table, precision=high)
    cos_part = parts[..., :x_modes]
    sin_part = parts[..., x_modes:]
    real_in = unfold_modes(
        cos_part[:, 0] - sin_part[:, 1], cos_part[:, 0] + sin_part[:, 1], half
    )
    imag_in = unfold_modes(
        cos_part[:, 1] + sin_part[:, 0], cos_part[:, 1] - sin_part[:, 0], half
    )
    spectra = jnp.stack([real_in, imag_in], axis=2)

    gathered = lax.all_to_all(spectra, "chan", split_axis=3, concat_axis=0, tiled=True)
    real_in = gathered[:, :, 0]
    imag_in = gathered[:, :, 1]
    real_out = jnp.einsum(
        "qpio,iqp->oqp", spectral_weight[0], real_in, precision=highest
    ) - jnp.einsum("qpio,iqp->oqp", spectral_weight[1], imag_in, precision=highest)
    imag_out = jnp.einsum(
        "qpio,iqp->oqp", spectral_weight[0], imag_in, precision=highest
    ) + jnp.einsum("qpio,iqp->oqp", spectral_weight[1], real_in, precision=highest)
    mixed = lax.all_to_all(
        jnp.stack([real_out, imag_out], axis=2), "chan", split_axis=0, concat_axis=3, tiled=True
    )

    real_pos, real_neg = fold_modes(mixed[:, :, 0], half)
    imag_pos, imag_neg = fold_modes(mixed[:, :, 1], half)
    pad = [(0, 0), (0, 0), (0, x_modes - half - 1)]
    coef_real = jnp.concatenate(
        [jnp.pad(real_pos + real_neg, pad), jnp.pad(imag_pos - imag_neg, pad)], axis=-1
    )
    coef_imag = jnp.concatenate(
        [jnp.pad(imag_pos + imag_neg, pad), jnp.pad(real_neg - real_pos, pad)], axis=-1
    )
    coef = jnp.stack([coef_real, coef_imag], axis=1)
    inverted = jnp.einsum("otqk,kx->otqx", coef, x_table, precision=high)
    inverted = windows(inverted, row_devices, row_count, halo)
    inverted = lax.all_to_all(inverted, "rows", split_axis=3, concat_axis=2, tiled=True)
    y_weights = jnp.where(jnp.arange(all_ymodes) == 0, 1.0, 2.0).astype(jnp.float32) * norm_scale
    inverted = inverted.reshape(local_chan, 2, all_ymodes, win_rows) * y_weights[:, None]
    inverted = inverted.reshape(local_chan, 2 * all_ymodes, win_rows)

    spectral = jnp.einsum("ckx,ky->cxy", inverted, table, precision=high)
    activated = jax.nn.gelu(
        spectral + skip_gain[:, None, None] * hidden_win + skip_bias[:, None, None],
        approximate=False,
    )
    partial_speed = jnp.sum(project_weight[:, :, None, None] * activated[None], axis=1)
    sent = windows(partial_speed, chan_devices, tile_cols, halo)
    sent = jnp.moveaxis(sent, 2, 0)
    chunk_shape = sent.shape[1:]
    chunk = math.prod(chunk_shape)
    lanes = 128
    flat_len = -(-chunk // lanes) * lanes
    flat = jnp.pad(sent.reshape(chan_devices, chunk), ((0, 0), (0, flat_len - chunk)))
    flat = flat.reshape(chan_devices, flat_len // lanes, lanes)
    received = lax.all_to_all(flat, "chan", split_axis=0, concat_axis=0, tiled=True)
    speed = jnp.sum(received, axis=0).reshape(-1)[:chunk].reshape(chunk_shape)
    speed = speed + project_bias[:, None, None]
    speed = speed * fields[2][None]
    velocity = speed[:, halo : halo + row_count, halo : halo + tile_cols]

    level = fields[0]
    band = fields[1]
    for level_step in range(LS_STEPS):
        inner = level_step + 1
        rows_end = win_rows - inner
        cols_end = tile_cols + 2 * halo - inner
        level = advance(
            level,
            speed[0, inner:rows_end, inner:cols_end],
            speed[1, inner:rows_end, inner:cols_end],
            band[inner:rows_end, inner:cols_end],
        )
    return (velocity, level)


def solution(mesh):
    return jax.shard_map(
        on_device,
        mesh=mesh,
        in_specs=(
            P("chan", "rows", None),
            P("rows", "chan"),
            P(None, "rows", "chan", None, None),
            P("chan"),
            P("chan"),
            P(None, "chan"),
            P(),
            P("rows", "chan"),
            P("rows", "chan"),
        ),
        out_specs=(P(None, "rows", "chan"), P("rows", "chan")),
        check_vma=False,
    )
```

```python
import math

import jax
import jax.numpy as jnp
from jax import lax
from jax.sharding import PartitionSpec as P

LS_STEPS = 4


time_step = 0.25
highest = lax.Precision.HIGHEST
high = lax.Precision.HIGH


def with_halo(block, sides, width):
    for axis, dim in sides:
        count = lax.axis_size(axis)
        forward = [(i, i + 1) for i in range(count - 1)]
        backward = [(target, source) for source, target in forward]
        low = lax.ppermute(
            lax.slice_in_dim(block, block.shape[dim] - width, None, axis=dim), axis, forward
        )
        high = lax.ppermute(lax.slice_in_dim(block, 0, width, axis=dim), axis, backward)
        block = jnp.concatenate([low, block, high], axis=dim)
    return block


def angles(freqs, places, length):
    product = freqs[:, None] * places[None, :] % length
    return 2.0 * math.pi / length * product.astype(jnp.float32)


def base_table(modes, length):
    phase = angles(jnp.arange(modes, dtype=jnp.int32), jnp.arange(length, dtype=jnp.int32), length)
    return jnp.concatenate([jnp.cos(phase), -jnp.sin(phase)])


def fold_modes(vec, half):
    pos = jnp.pad(vec[..., :half], [(0, 0)] * (vec.ndim - 1) + [(0, 1)])
    neg = jnp.pad(jnp.flip(vec[..., half:], -1), [(0, 0)] * (vec.ndim - 1) + [(1, 0)])
    return pos, neg


def unfold_modes(plus, minus, half):
    return jnp.concatenate([plus[..., :half], jnp.flip(minus[..., 1 : half + 1], -1)], axis=-1)


def windows(block, count, size, halo):
    padded = jnp.pad(block, [(0, 0)] * (block.ndim - 1) + [(halo, size)])
    lead = block.shape[:-1]
    main = padded[..., : count * size].reshape(lead + (count, size))
    tail = padded[..., size : size + count * size].reshape(lead + (count, size))
    return jnp.concatenate([main, tail[..., : 2 * halo]], axis=-1)


def halo_2d(block, width):
    n_rows = lax.axis_size("rows")
    n_chan = lax.axis_size("chan")

    def shifted(piece, d_row, d_chan):
        pairs = [
            (r * n_chan + c, (r + d_row) * n_chan + c + d_chan)
            for r in range(n_rows)
            for c in range(n_chan)
            if 0 <= r + d_row < n_rows and 0 <= c + d_chan < n_chan
        ]
        return lax.ppermute(piece, ("rows", "chan"), pairs)

    lo, hi = slice(-width, None), slice(0, width)
    every = slice(None)
    parts = {}
    for d_row, rows in ((1, lo), (0, every), (-1, hi)):
        for d_chan, cols in ((1, lo), (0, every), (-1, hi)):
            piece = block[..., rows, cols]
            parts[d_row, d_chan] = piece if d_row == d_chan == 0 else shifted(piece, d_row, d_chan)
    bands = [
        jnp.concatenate([parts[d_row, 1], parts[d_row, 0], parts[d_row, -1]], axis=-1)
        for d_row in (1, 0, -1)
    ]
    return jnp.concatenate(bands, axis=-2)


def rows_halo_pair(first, second, width, second_width):
    count = lax.axis_size("rows")
    forward = [(i, i + 1) for i in range(count - 1)]
    backward = [(target, source) for source, target in forward]

    def packed(rows, second_rows):
        a, b = first[..., rows, :], second[..., second_rows, :]
        return jnp.concatenate([a.reshape(-1), b.reshape(-1)]), a.shape, b.shape

    def unpacked(flat, a_shape, b_shape):
        split = math.prod(a_shape)
        return flat[:split].reshape(a_shape), flat[split:].reshape(b_shape)

    low, a_shape, b_shape = packed(slice(-width, None), slice(-second_width, None))
    high, _, _ = packed(slice(0, width), slice(0, second_width))
    low_a, low_b = unpacked(lax.ppermute(low, "rows", forward), a_shape, b_shape)
    high_a, high_b = unpacked(lax.ppermute(high, "rows", backward), a_shape, b_shape)
    return (
        jnp.concatenate([low_a, first, high_a], axis=-2),
        jnp.concatenate([low_b, second, high_b], axis=-2),
    )


def advance(padded, speed_x, speed_y, band):
    center = padded[1:-1, 1:-1]
    back_x = center - padded[:-2, 1:-1]
    ahead_x = padded[2:, 1:-1] - center
    back_y = center - padded[1:-1, :-2]
    ahead_y = padded[1:-1, 2:] - center
    transport = jnp.maximum(speed_x, 0.0) * back_x + jnp.minimum(speed_x, 0.0) * ahead_x
    transport = transport + jnp.maximum(speed_y, 0.0) * back_y + jnp.minimum(speed_y, 0.0) * ahead_y
    return center - time_step * band * transport


def on_device(
    hidden,
    front,
    spectral_weight,
    skip_gain,
    skip_bias,
    project_weight,
    project_bias,
    ice_mask,
    front_flags,
):
    halo = LS_STEPS
    speed_halo = LS_STEPS - 1
    local_chan, row_count, columns = hidden.shape
    row_devices = lax.axis_size("rows")
    chan_devices = lax.axis_size("chan")
    local_ymodes = spectral_weight.shape[1]
    all_rows = row_count * row_devices
    all_xmodes = spectral_weight.shape[2] * chan_devices
    all_ymodes = local_ymodes * row_devices
    tile_cols = columns // chan_devices
    win_rows = row_count + 2 * speed_halo
    norm_scale = 1.0 / math.sqrt(all_rows * columns * all_xmodes * all_ymodes)

    fields = jnp.stack(
        [front, front_flags.astype(jnp.float32), ice_mask.astype(jnp.float32)]
    )

    table = base_table(all_ymodes, columns)
    half = all_xmodes // 2
    if all_rows == columns and all_ymodes > half:
        x_table = table
    else:
        x_table = base_table(half + 1, all_rows)
    x_modes = x_table.shape[0] // 2

    spec_y = jnp.einsum("cxy,ky->ckx", hidden, table, precision=high)
    spec_y = spec_y.reshape(local_chan, 2, all_ymodes, row_count)
    by_freq = lax.all_to_all(spec_y, "rows", split_axis=2, concat_axis=3, tiled=True)
    hidden_late, fields, by_freq = lax.optimization_barrier((hidden, fields, by_freq))
    hidden_win, fields = rows_halo_pair(hidden_late, fields, speed_halo, halo)
    fields = with_halo(fields, (("chan", 2),), halo)
    fields, hidden_win = lax.optimization_barrier((fields, hidden_win))
    parts = jnp.einsum("caqx,kx->caqk", by_freq, x_table, precision=high)
    cos_part = parts[..., :x_modes]
    sin_part = parts[..., x_modes:]
    real_in = unfold_modes(
        cos_part[:, 0] - sin_part[:, 1], cos_part[:, 0] + sin_part[:, 1], half
    )
    imag_in = unfold_modes(
        cos_part[:, 1] + sin_part[:, 0], cos_part[:, 1] - sin_part[:, 0], half
    )
    spectra = jnp.stack([real_in, imag_in], axis=2)

    gathered = lax.all_to_all(spectra, "chan", split_axis=3, concat_axis=0, tiled=True)
    real_in = gathered[:, :, 0]
    imag_in = gathered[:, :, 1]
    real_out = jnp.einsum(
        "qpio,iqp->oqp", spectral_weight[0], real_in, precision=highest
    ) - jnp.einsum("qpio,iqp->oqp", spectral_weight[1], imag_in, precision=highest)
    imag_out = jnp.einsum(
        "qpio,iqp->oqp", spectral_weight[0], imag_in, precision=highest
    ) + jnp.einsum("qpio,iqp->oqp", spectral_weight[1], real_in, precision=highest)
    mixed = lax.all_to_all(
        jnp.stack([real_out, imag_out], axis=2), "chan", split_axis=0, concat_axis=3, tiled=True
    )

    real_pos, real_neg = fold_modes(mixed[:, :, 0], half)
    imag_pos, imag_neg = fold_modes(mixed[:, :, 1], half)
    pad = [(0, 0), (0, 0), (0, x_modes - half - 1)]
    coef_real = jnp.concatenate(
        [jnp.pad(real_pos + real_neg, pad), jnp.pad(imag_pos - imag_neg, pad)], axis=-1
    )
    coef_imag = jnp.concatenate(
        [jnp.pad(imag_pos + imag_neg, pad), jnp.pad(real_neg - real_pos, pad)], axis=-1
    )
    coef = jnp.stack([coef_real, coef_imag], axis=1)
    inverted = jnp.einsum("otqk,kx->otqx", coef, x_table, precision=high)
    inverted = windows(inverted, row_devices, row_count, speed_halo)
    inverted = lax.all_to_all(inverted, "rows", split_axis=3, concat_axis=2, tiled=True)
    y_weights = jnp.where(jnp.arange(all_ymodes) == 0, 1.0, 2.0).astype(jnp.float32) * norm_scale
    inverted = inverted.reshape(local_chan, 2, all_ymodes, win_rows) * y_weights[:, None]
    inverted = inverted.reshape(local_chan, 2 * all_ymodes, win_rows)

    spectral = jnp.einsum("ckx,ky->cxy", inverted, table, precision=high)
    activated = jax.nn.gelu(
        spectral + skip_gain[:, None, None] * hidden_win + skip_bias[:, None, None],
        approximate=False,
    )
    partial_speed = jnp.sum(project_weight[:, :, None, None] * activated[None], axis=1)
    sent = windows(partial_speed, chan_devices, tile_cols, speed_halo)
    sent = jnp.moveaxis(sent, 2, 0)
    chunk_shape = sent.shape[1:]
    chunk = math.prod(chunk_shape)
    lanes = 128
    flat_len = -(-chunk // lanes) * lanes
    flat = jnp.pad(sent.reshape(chan_devices, chunk), ((0, 0), (0, flat_len - chunk)))
    flat = flat.reshape(chan_devices, flat_len // lanes, lanes)
    received = lax.all_to_all(flat, "chan", split_axis=0, concat_axis=0, tiled=True)
    speed = jnp.sum(received, axis=0).reshape(-1)[:chunk].reshape(chunk_shape)
    speed = speed + project_bias[:, None, None]
    speed = speed * fields[2][None, 1:-1, 1:-1]
    velocity = speed[:, speed_halo : speed_halo + row_count, speed_halo : speed_halo + tile_cols]

    level = fields[0]
    band = fields[1][1:-1, 1:-1]
    speed_rows, speed_cols = band.shape
    for level_step in range(LS_STEPS):
        rows_end = speed_rows - level_step
        cols_end = speed_cols - level_step
        level = advance(
            level,
            speed[0, level_step:rows_end, level_step:cols_end],
            speed[1, level_step:rows_end, level_step:cols_end],
            band[level_step:rows_end, level_step:cols_end],
        )
    return (velocity, level)


def solution(mesh):
    return jax.shard_map(
        on_device,
        mesh=mesh,
        in_specs=(
            P("chan", "rows", None),
            P("rows", "chan"),
            P(None, "rows", "chan", None, None),
            P("chan"),
            P("chan"),
            P(None, "chan"),
            P(),
            P("rows", "chan"),
            P("rows", "chan"),
        ),
        out_specs=(P(None, "rows", "chan"), P("rows", "chan")),
        check_vma=False,
    )
```

```python
import math

import jax
import jax.numpy as jnp
from jax import lax
from jax.sharding import PartitionSpec as P

LS_STEPS = 4


time_step = 0.25
highest = lax.Precision.HIGHEST
high = lax.Precision.HIGH


def with_halo(block, sides, width):
    for axis, dim in sides:
        count = lax.axis_size(axis)
        forward = [(i, i + 1) for i in range(count - 1)]
        backward = [(target, source) for source, target in forward]
        low = lax.ppermute(
            lax.slice_in_dim(block, block.shape[dim] - width, None, axis=dim), axis, forward
        )
        high = lax.ppermute(lax.slice_in_dim(block, 0, width, axis=dim), axis, backward)
        block = jnp.concatenate([low, block, high], axis=dim)
    return block


def angles(freqs, places, length):
    product = freqs[:, None] * places[None, :] % length
    return 2.0 * math.pi / length * product.astype(jnp.float32)


def base_table(modes, length):
    lanes = 128 if length % 128 == 0 else length
    ids = jnp.arange(modes, dtype=jnp.int32)
    coarse = angles(ids, jnp.arange(length // lanes, dtype=jnp.int32) * lanes, length)
    fine = angles(ids, jnp.arange(lanes, dtype=jnp.int32), length)
    cos_hi, sin_hi = jnp.cos(coarse)[:, :, None], jnp.sin(coarse)[:, :, None]
    cos_lo, sin_lo = jnp.cos(fine)[:, None, :], jnp.sin(fine)[:, None, :]
    cos_all = (cos_hi * cos_lo - sin_hi * sin_lo).reshape(modes, length)
    sin_all = (sin_hi * cos_lo + cos_hi * sin_lo).reshape(modes, length)
    return jnp.concatenate([cos_all, -sin_all])


def fold_modes(vec, half):
    pos = jnp.pad(vec[..., :half], [(0, 0)] * (vec.ndim - 1) + [(0, 1)])
    neg = jnp.pad(jnp.flip(vec[..., half:], -1), [(0, 0)] * (vec.ndim - 1) + [(1, 0)])
    return pos, neg


def unfold_modes(plus, minus, half):
    return jnp.concatenate([plus[..., :half], jnp.flip(minus[..., 1 : half + 1], -1)], axis=-1)


def windows(block, count, size, halo):
    padded = jnp.pad(block, [(0, 0)] * (block.ndim - 1) + [(halo, size)])
    lead = block.shape[:-1]
    main = padded[..., : count * size].reshape(lead + (count, size))
    tail = padded[..., size : size + count * size].reshape(lead + (count, size))
    return jnp.concatenate([main, tail[..., : 2 * halo]], axis=-1)


def halo_2d(block, width):
    n_rows = lax.axis_size("rows")
    n_chan = lax.axis_size("chan")

    def shifted(piece, d_row, d_chan):
        pairs = [
            (r * n_chan + c, (r + d_row) * n_chan + c + d_chan)
            for r in range(n_rows)
            for c in range(n_chan)
            if 0 <= r + d_row < n_rows and 0 <= c + d_chan < n_chan
        ]
        return lax.ppermute(piece, ("rows", "chan"), pairs)

    lo, hi = slice(-width, None), slice(0, width)
    every = slice(None)
    parts = {}
    for d_row, rows in ((1, lo), (0, every), (-1, hi)):
        for d_chan, cols in ((1, lo), (0, every), (-1, hi)):
            piece = block[..., rows, cols]
            parts[d_row, d_chan] = piece if d_row == d_chan == 0 else shifted(piece, d_row, d_chan)
    bands = [
        jnp.concatenate([parts[d_row, 1], parts[d_row, 0], parts[d_row, -1]], axis=-1)
        for d_row in (1, 0, -1)
    ]
    return jnp.concatenate(bands, axis=-2)


def rows_halo_pair(first, second, width):
    count = lax.axis_size("rows")
    forward = [(i, i + 1) for i in range(count - 1)]
    backward = [(target, source) for source, target in forward]

    def packed(rows):
        a, b = first[..., rows, :], second[..., rows, :]
        return jnp.concatenate([a.reshape(-1), b.reshape(-1)]), a.shape, b.shape

    def unpacked(flat, a_shape, b_shape):
        split = math.prod(a_shape)
        return flat[:split].reshape(a_shape), flat[split:].reshape(b_shape)

    low, a_shape, b_shape = packed(slice(-width, None))
    high, _, _ = packed(slice(0, width))
    low_a, low_b = unpacked(lax.ppermute(low, "rows", forward), a_shape, b_shape)
    high_a, high_b = unpacked(lax.ppermute(high, "rows", backward), a_shape, b_shape)
    return (
        jnp.concatenate([low_a, first, high_a], axis=-2),
        jnp.concatenate([low_b, second, high_b], axis=-2),
    )


def advance(padded, speed_x, speed_y, band):
    center = padded[1:-1, 1:-1]
    back_x = center - padded[:-2, 1:-1]
    ahead_x = padded[2:, 1:-1] - center
    back_y = center - padded[1:-1, :-2]
    ahead_y = padded[1:-1, 2:] - center
    transport = jnp.maximum(speed_x, 0.0) * back_x + jnp.minimum(speed_x, 0.0) * ahead_x
    transport = transport + jnp.maximum(speed_y, 0.0) * back_y + jnp.minimum(speed_y, 0.0) * ahead_y
    return center - time_step * band * transport


def on_device(
    hidden,
    front,
    spectral_weight,
    skip_gain,
    skip_bias,
    project_weight,
    project_bias,
    ice_mask,
    front_flags,
):
    halo = LS_STEPS
    local_chan, row_count, columns = hidden.shape
    row_devices = lax.axis_size("rows")
    chan_devices = lax.axis_size("chan")
    local_ymodes = spectral_weight.shape[1]
    all_rows = row_count * row_devices
    all_xmodes = spectral_weight.shape[2] * chan_devices
    all_ymodes = local_ymodes * row_devices
    tile_cols = columns // chan_devices
    win_rows = row_count + 2 * halo
    norm_scale = 1.0 / math.sqrt(all_rows * columns * all_xmodes * all_ymodes)

    fields = jnp.stack(
        [front, front_flags.astype(jnp.float32), ice_mask.astype(jnp.float32)]
    )

    table = base_table(all_ymodes, columns)
    half = all_xmodes // 2
    if all_rows == columns and all_ymodes > half:
        x_table = table
    else:
        x_table = base_table(half + 1, all_rows)
    x_modes = x_table.shape[0] // 2

    spec_y = jnp.einsum("cxy,ky->ckx", hidden, table, precision=high)
    spec_y = spec_y.reshape(local_chan, 2, all_ymodes, row_count)
    by_freq = lax.all_to_all(spec_y, "rows", split_axis=2, concat_axis=3, tiled=True)
    hidden_late, fields, by_freq = lax.optimization_barrier((hidden, fields, by_freq))
    hidden_win, fields = rows_halo_pair(hidden_late, fields, halo)
    fields = with_halo(fields, (("chan", 2),), halo)
    fields, hidden_win = lax.optimization_barrier((fields, hidden_win))
    parts = jnp.einsum("caqx,kx->caqk", by_freq, x_table, precision=high)
    cos_part = parts[..., :x_modes]
    sin_part = parts[..., x_modes:]
    real_in = unfold_modes(
        cos_part[:, 0] - sin_part[:, 1], cos_part[:, 0] + sin_part[:, 1], half
    )
    imag_in = unfold_modes(
        cos_part[:, 1] + sin_part[:, 0], cos_part[:, 1] - sin_part[:, 0], half
    )
    spectra = jnp.stack([real_in, imag_in], axis=2)

    gathered = lax.all_to_all(spectra, "chan", split_axis=3, concat_axis=0, tiled=True)
    real_in = gathered[:, :, 0]
    imag_in = gathered[:, :, 1]
    real_out = jnp.einsum(
        "qpio,iqp->oqp", spectral_weight[0], real_in, precision=highest
    ) - jnp.einsum("qpio,iqp->oqp", spectral_weight[1], imag_in, precision=highest)
    imag_out = jnp.einsum(
        "qpio,iqp->oqp", spectral_weight[0], imag_in, precision=highest
    ) + jnp.einsum("qpio,iqp->oqp", spectral_weight[1], real_in, precision=highest)
    mixed = lax.all_to_all(
        jnp.stack([real_out, imag_out], axis=2), "chan", split_axis=0, concat_axis=3, tiled=True
    )

    real_pos, real_neg = fold_modes(mixed[:, :, 0], half)
    imag_pos, imag_neg = fold_modes(mixed[:, :, 1], half)
    pad = [(0, 0), (0, 0), (0, x_modes - half - 1)]
    coef_real = jnp.concatenate(
        [jnp.pad(real_pos + real_neg, pad), jnp.pad(imag_pos - imag_neg, pad)], axis=-1
    )
    coef_imag = jnp.concatenate(
        [jnp.pad(imag_pos + imag_neg, pad), jnp.pad(real_neg - real_pos, pad)], axis=-1
    )
    coef = jnp.stack([coef_real, coef_imag], axis=1)
    inverted = jnp.einsum("otqk,kx->otqx", coef, x_table, precision=high)
    inverted = windows(inverted, row_devices, row_count, halo)
    inverted = lax.all_to_all(inverted, "rows", split_axis=3, concat_axis=2, tiled=True)
    y_weights = jnp.where(jnp.arange(all_ymodes) == 0, 1.0, 2.0).astype(jnp.float32) * norm_scale
    inverted = inverted.reshape(local_chan, 2, all_ymodes, win_rows) * y_weights[:, None]
    inverted = inverted.reshape(local_chan, 2 * all_ymodes, win_rows)

    spectral = jnp.einsum("ckx,ky->cxy", inverted, table, precision=high)
    activated = jax.nn.gelu(
        spectral + skip_gain[:, None, None] * hidden_win + skip_bias[:, None, None],
        approximate=False,
    )
    partial_speed = jnp.sum(project_weight[:, :, None, None] * activated[None], axis=1)
    sent = windows(partial_speed, chan_devices, tile_cols, halo)
    sent = jnp.moveaxis(sent, 2, 0)
    chunk_shape = sent.shape[1:]
    chunk = math.prod(chunk_shape)
    lanes = 128
    flat_len = -(-chunk // lanes) * lanes
    flat = jnp.pad(sent.reshape(chan_devices, chunk), ((0, 0), (0, flat_len - chunk)))
    flat = flat.reshape(chan_devices, flat_len // lanes, lanes)
    received = lax.all_to_all(flat, "chan", split_axis=0, concat_axis=0, tiled=True)
    speed = jnp.sum(received, axis=0).reshape(-1)[:chunk].reshape(chunk_shape)
    speed = speed + project_bias[:, None, None]
    speed = speed * fields[2][None]
    velocity = speed[:, halo : halo + row_count, halo : halo + tile_cols]

    level = fields[0]
    band = fields[1]
    for level_step in range(LS_STEPS):
        inner = level_step + 1
        rows_end = win_rows - inner
        cols_end = tile_cols + 2 * halo - inner
        level = advance(
            level,
            speed[0, inner:rows_end, inner:cols_end],
            speed[1, inner:rows_end, inner:cols_end],
            band[inner:rows_end, inner:cols_end],
        )
    return (velocity, level)


def solution(mesh):
    return jax.shard_map(
        on_device,
        mesh=mesh,
        in_specs=(
            P("chan", "rows", None),
            P("rows", "chan"),
            P(None, "rows", "chan", None, None),
            P("chan"),
            P("chan"),
            P(None, "chan"),
            P(),
            P("rows", "chan"),
            P("rows", "chan"),
        ),
        out_specs=(P(None, "rows", "chan"), P("rows", "chan")),
        check_vma=False,
    )
```

```python
import math

import jax
import jax.numpy as jnp
from jax import lax
from jax.sharding import PartitionSpec as P

LS_STEPS = 4


time_step = 0.25
highest = lax.Precision.HIGHEST
high = lax.Precision.HIGH


def with_halo(block, sides, width):
    for axis, dim in sides:
        count = lax.axis_size(axis)
        forward = [(i, i + 1) for i in range(count - 1)]
        backward = [(target, source) for source, target in forward]
        low = lax.ppermute(
            lax.slice_in_dim(block, block.shape[dim] - width, None, axis=dim), axis, forward
        )
        high = lax.ppermute(lax.slice_in_dim(block, 0, width, axis=dim), axis, backward)
        block = jnp.concatenate([low, block, high], axis=dim)
    return block


def angles(freqs, places, length):
    product = freqs[:, None] * places[None, :] % length
    return 2.0 * math.pi / length * product.astype(jnp.float32)


def base_table(modes, length):
    lanes = 128 if length % 128 == 0 else length
    ids = jnp.arange(modes, dtype=jnp.int32)
    coarse = angles(ids, jnp.arange(length // lanes, dtype=jnp.int32) * lanes, length)
    fine = angles(ids, jnp.arange(lanes, dtype=jnp.int32), length)
    cos_hi, sin_hi = jnp.cos(coarse)[:, :, None], jnp.sin(coarse)[:, :, None]
    cos_lo, sin_lo = jnp.cos(fine)[:, None, :], jnp.sin(fine)[:, None, :]
    cos_all = (cos_hi * cos_lo - sin_hi * sin_lo).reshape(modes, length)
    sin_all = (sin_hi * cos_lo + cos_hi * sin_lo).reshape(modes, length)
    return jnp.concatenate([cos_all, -sin_all])


def fold_modes(vec, half):
    pos = jnp.pad(vec[..., :half], [(0, 0)] * (vec.ndim - 1) + [(0, 1)])
    neg = jnp.pad(jnp.flip(vec[..., half:], -1), [(0, 0)] * (vec.ndim - 1) + [(1, 0)])
    return pos, neg


def unfold_modes(plus, minus, half):
    return jnp.concatenate([plus[..., :half], jnp.flip(minus[..., 1 : half + 1], -1)], axis=-1)


def windows(block, count, size, halo):
    padded = jnp.pad(block, [(0, 0)] * (block.ndim - 1) + [(halo, size)])
    lead = block.shape[:-1]
    main = padded[..., : count * size].reshape(lead + (count, size))
    tail = padded[..., size : size + count * size].reshape(lead + (count, size))
    return jnp.concatenate([main, tail[..., : 2 * halo]], axis=-1)


def halo_2d(block, width):
    n_rows = lax.axis_size("rows")
    n_chan = lax.axis_size("chan")

    def shifted(piece, d_row, d_chan):
        pairs = [
            (r * n_chan + c, (r + d_row) * n_chan + c + d_chan)
            for r in range(n_rows)
            for c in range(n_chan)
            if 0 <= r + d_row < n_rows and 0 <= c + d_chan < n_chan
        ]
        return lax.ppermute(piece, ("rows", "chan"), pairs)

    lo, hi = slice(-width, None), slice(0, width)
    every = slice(None)
    parts = {}
    for d_row, rows in ((1, lo), (0, every), (-1, hi)):
        for d_chan, cols in ((1, lo), (0, every), (-1, hi)):
            piece = block[..., rows, cols]
            parts[d_row, d_chan] = piece if d_row == d_chan == 0 else shifted(piece, d_row, d_chan)
    bands = [
        jnp.concatenate([parts[d_row, 1], parts[d_row, 0], parts[d_row, -1]], axis=-1)
        for d_row in (1, 0, -1)
    ]
    return jnp.concatenate(bands, axis=-2)


def rows_halo_pair(first, second, width):
    count = lax.axis_size("rows")
    forward = [(i, i + 1) for i in range(count - 1)]
    backward = [(target, source) for source, target in forward]

    def packed(rows):
        a, b = first[..., rows, :], second[..., rows, :]
        return jnp.concatenate([a.reshape(-1), b.reshape(-1)]), a.shape, b.shape

    def unpacked(flat, a_shape, b_shape):
        split = math.prod(a_shape)
        return flat[:split].reshape(a_shape), flat[split:].reshape(b_shape)

    low, a_shape, b_shape = packed(slice(-width, None))
    high, _, _ = packed(slice(0, width))
    low_a, low_b = unpacked(lax.ppermute(low, "rows", forward), a_shape, b_shape)
    high_a, high_b = unpacked(lax.ppermute(high, "rows", backward), a_shape, b_shape)
    return (
        jnp.concatenate([low_a, first, high_a], axis=-2),
        jnp.concatenate([low_b, second, high_b], axis=-2),
    )


def advance(padded, speed_x, speed_y, band):
    center = padded[1:-1, 1:-1]
    back_x = center - padded[:-2, 1:-1]
    ahead_x = padded[2:, 1:-1] - center
    back_y = center - padded[1:-1, :-2]
    ahead_y = padded[1:-1, 2:] - center
    transport = jnp.maximum(speed_x, 0.0) * back_x + jnp.minimum(speed_x, 0.0) * ahead_x
    transport = transport + jnp.maximum(speed_y, 0.0) * back_y + jnp.minimum(speed_y, 0.0) * ahead_y
    return center - time_step * band * transport


def on_device(
    hidden,
    front,
    spectral_weight,
    skip_gain,
    skip_bias,
    project_weight,
    project_bias,
    ice_mask,
    front_flags,
):
    halo = LS_STEPS
    local_chan, row_count, columns = hidden.shape
    row_devices = lax.axis_size("rows")
    chan_devices = lax.axis_size("chan")
    local_ymodes = spectral_weight.shape[1]
    all_rows = row_count * row_devices
    all_xmodes = spectral_weight.shape[2] * chan_devices
    all_ymodes = local_ymodes * row_devices
    tile_cols = columns // chan_devices
    win_rows = row_count + 2 * halo
    norm_scale = 1.0 / math.sqrt(all_rows * columns * all_xmodes * all_ymodes)

    fields = jnp.stack(
        [front, front_flags.astype(jnp.float32), ice_mask.astype(jnp.float32)]
    )

    table = base_table(all_ymodes, columns)
    half = all_xmodes // 2
    if all_rows == columns and all_ymodes > half:
        x_table = table
    else:
        x_table = base_table(half + 1, all_rows)
    x_modes = x_table.shape[0] // 2

    spec_y = jnp.einsum("cxy,ky->ckx", hidden, table, precision=high)
    spec_y = spec_y.reshape(local_chan, 2, row_devices, local_ymodes, row_count)
    by_freq = lax.all_to_all(spec_y, "rows", split_axis=2, concat_axis=0, tiled=False)
    hidden_late, fields, by_freq = lax.optimization_barrier((hidden, fields, by_freq))
    hidden_win, fields = rows_halo_pair(hidden_late, fields, halo)
    fields = with_halo(fields, (("chan", 2),), halo)
    fields, hidden_win = lax.optimization_barrier((fields, hidden_win))
    blocked_table = x_table.reshape(x_table.shape[0], row_devices, row_count)
    parts = jnp.einsum("scaqx,ksx->caqk", by_freq, blocked_table, precision=high)
    cos_part = parts[..., :x_modes]
    sin_part = parts[..., x_modes:]
    real_in = unfold_modes(
        cos_part[:, 0] - sin_part[:, 1], cos_part[:, 0] + sin_part[:, 1], half
    )
    imag_in = unfold_modes(
        cos_part[:, 1] + sin_part[:, 0], cos_part[:, 1] - sin_part[:, 0], half
    )
    spectra = jnp.stack([real_in, imag_in], axis=2)

    gathered = lax.all_to_all(spectra, "chan", split_axis=3, concat_axis=0, tiled=True)
    real_in = gathered[:, :, 0]
    imag_in = gathered[:, :, 1]
    real_out = jnp.einsum(
        "qpio,iqp->oqp", spectral_weight[0], real_in, precision=highest
    ) - jnp.einsum("qpio,iqp->oqp", spectral_weight[1], imag_in, precision=highest)
    imag_out = jnp.einsum(
        "qpio,iqp->oqp", spectral_weight[0], imag_in, precision=highest
    ) + jnp.einsum("qpio,iqp->oqp", spectral_weight[1], real_in, precision=highest)
    mixed = lax.all_to_all(
        jnp.stack([real_out, imag_out], axis=2), "chan", split_axis=0, concat_axis=3, tiled=True
    )

    real_pos, real_neg = fold_modes(mixed[:, :, 0], half)
    imag_pos, imag_neg = fold_modes(mixed[:, :, 1], half)
    pad = [(0, 0), (0, 0), (0, x_modes - half - 1)]
    coef_real = jnp.concatenate(
        [jnp.pad(real_pos + real_neg, pad), jnp.pad(imag_pos - imag_neg, pad)], axis=-1
    )
    coef_imag = jnp.concatenate(
        [jnp.pad(imag_pos + imag_neg, pad), jnp.pad(real_neg - real_pos, pad)], axis=-1
    )
    coef = jnp.stack([coef_real, coef_imag], axis=1)
    inverted = jnp.einsum("otqk,kx->otqx", coef, x_table, precision=high)
    inverted = windows(inverted, row_devices, row_count, halo)
    inverted = lax.all_to_all(inverted, "rows", split_axis=3, concat_axis=2, tiled=True)
    y_weights = jnp.where(jnp.arange(all_ymodes) == 0, 1.0, 2.0).astype(jnp.float32) * norm_scale
    inverted = inverted.reshape(local_chan, 2, all_ymodes, win_rows) * y_weights[:, None]
    inverted = inverted.reshape(local_chan, 2 * all_ymodes, win_rows)

    spectral = jnp.einsum("ckx,ky->cxy", inverted, table, precision=high)
    activated = jax.nn.gelu(
        spectral + skip_gain[:, None, None] * hidden_win + skip_bias[:, None, None],
        approximate=False,
    )
    partial_speed = jnp.sum(project_weight[:, :, None, None] * activated[None], axis=1)
    sent = windows(partial_speed, chan_devices, tile_cols, halo)
    sent = jnp.moveaxis(sent, 2, 0)
    chunk_shape = sent.shape[1:]
    chunk = math.prod(chunk_shape)
    lanes = 128
    flat_len = -(-chunk // lanes) * lanes
    flat = jnp.pad(sent.reshape(chan_devices, chunk), ((0, 0), (0, flat_len - chunk)))
    flat = flat.reshape(chan_devices, flat_len // lanes, lanes)
    received = lax.all_to_all(flat, "chan", split_axis=0, concat_axis=0, tiled=True)
    speed = jnp.sum(received, axis=0).reshape(-1)[:chunk].reshape(chunk_shape)
    speed = speed + project_bias[:, None, None]
    speed = speed * fields[2][None]
    velocity = speed[:, halo : halo + row_count, halo : halo + tile_cols]

    level = fields[0]
    band = fields[1]
    for level_step in range(LS_STEPS):
        inner = level_step + 1
        rows_end = win_rows - inner
        cols_end = tile_cols + 2 * halo - inner
        level = advance(
            level,
            speed[0, inner:rows_end, inner:cols_end],
            speed[1, inner:rows_end, inner:cols_end],
            band[inner:rows_end, inner:cols_end],
        )
    return (velocity, level)


def solution(mesh):
    return jax.shard_map(
        on_device,
        mesh=mesh,
        in_specs=(
            P("chan", "rows", None),
            P("rows", "chan"),
            P(None, "rows", "chan", None, None),
            P("chan"),
            P("chan"),
            P(None, "chan"),
            P(),
            P("rows", "chan"),
            P("rows", "chan"),
        ),
        out_specs=(P(None, "rows", "chan"), P("rows", "chan")),
        check_vma=False,
    )
```

```python
import math

import jax
import jax.numpy as jnp
from jax import lax
from jax.sharding import PartitionSpec as P

LS_STEPS = 4


time_step = 0.25
highest = lax.Precision.HIGHEST
high = lax.Precision.HIGH


def with_halo(block, sides, width):
    for axis, dim in sides:
        count = lax.axis_size(axis)
        forward = [(i, i + 1) for i in range(count - 1)]
        backward = [(target, source) for source, target in forward]
        low = lax.ppermute(
            lax.slice_in_dim(block, block.shape[dim] - width, None, axis=dim), axis, forward
        )
        high = lax.ppermute(lax.slice_in_dim(block, 0, width, axis=dim), axis, backward)
        block = jnp.concatenate([low, block, high], axis=dim)
    return block


def angles(freqs, places, length):
    product = freqs[:, None] * places[None, :] % length
    return 2.0 * math.pi / length * product.astype(jnp.float32)


def base_table(modes, length):
    lanes = 128 if length % 128 == 0 else length
    ids = jnp.arange(modes, dtype=jnp.int32)
    coarse = angles(ids, jnp.arange(length // lanes, dtype=jnp.int32) * lanes, length)
    fine = angles(ids, jnp.arange(lanes, dtype=jnp.int32), length)
    cos_hi, sin_hi = jnp.cos(coarse)[:, :, None], jnp.sin(coarse)[:, :, None]
    cos_lo, sin_lo = jnp.cos(fine)[:, None, :], jnp.sin(fine)[:, None, :]
    cos_all = (cos_hi * cos_lo - sin_hi * sin_lo).reshape(modes, length)
    sin_all = (sin_hi * cos_lo + cos_hi * sin_lo).reshape(modes, length)
    return jnp.concatenate([cos_all, -sin_all])


def fold_modes(vec, half):
    pos = jnp.pad(vec[..., :half], [(0, 0)] * (vec.ndim - 1) + [(0, 1)])
    neg = jnp.pad(jnp.flip(vec[..., half:], -1), [(0, 0)] * (vec.ndim - 1) + [(1, 0)])
    return pos, neg


def unfold_modes(plus, minus, half):
    return jnp.concatenate([plus[..., :half], jnp.flip(minus[..., 1 : half + 1], -1)], axis=-1)


def windows(block, count, size, halo):
    padded = jnp.pad(block, [(0, 0)] * (block.ndim - 1) + [(halo, size)])
    lead = block.shape[:-1]
    main = padded[..., : count * size].reshape(lead + (count, size))
    tail = padded[..., size : size + count * size].reshape(lead + (count, size))
    return jnp.concatenate([main, tail[..., : 2 * halo]], axis=-1)


def halo_2d(block, width):
    n_rows = lax.axis_size("rows")
    n_chan = lax.axis_size("chan")

    def shifted(piece, d_row, d_chan):
        pairs = [
            (r * n_chan + c, (r + d_row) * n_chan + c + d_chan)
            for r in range(n_rows)
            for c in range(n_chan)
            if 0 <= r + d_row < n_rows and 0 <= c + d_chan < n_chan
        ]
        return lax.ppermute(piece, ("rows", "chan"), pairs)

    lo, hi = slice(-width, None), slice(0, width)
    every = slice(None)
    parts = {}
    for d_row, rows in ((1, lo), (0, every), (-1, hi)):
        for d_chan, cols in ((1, lo), (0, every), (-1, hi)):
            piece = block[..., rows, cols]
            parts[d_row, d_chan] = piece if d_row == d_chan == 0 else shifted(piece, d_row, d_chan)
    bands = [
        jnp.concatenate([parts[d_row, 1], parts[d_row, 0], parts[d_row, -1]], axis=-1)
        for d_row in (1, 0, -1)
    ]
    return jnp.concatenate(bands, axis=-2)


def rows_halo_pair(first, second, width):
    count = lax.axis_size("rows")
    forward = [(i, i + 1) for i in range(count - 1)]
    backward = [(target, source) for source, target in forward]

    def packed(rows):
        a, b = first[..., rows, :], second[..., rows, :]
        return jnp.concatenate([a.reshape(-1), b.reshape(-1)]), a.shape, b.shape

    def unpacked(flat, a_shape, b_shape):
        split = math.prod(a_shape)
        return flat[:split].reshape(a_shape), flat[split:].reshape(b_shape)

    low, a_shape, b_shape = packed(slice(-width, None))
    high, _, _ = packed(slice(0, width))
    low_a, low_b = unpacked(lax.ppermute(low, "rows", forward), a_shape, b_shape)
    high_a, high_b = unpacked(lax.ppermute(high, "rows", backward), a_shape, b_shape)
    return (
        jnp.concatenate([low_a, first, high_a], axis=-2),
        jnp.concatenate([low_b, second, high_b], axis=-2),
    )


def advance(padded, speed_x, speed_y, band):
    center = padded[1:-1, 1:-1]
    back_x = center - padded[:-2, 1:-1]
    ahead_x = padded[2:, 1:-1] - center
    back_y = center - padded[1:-1, :-2]
    ahead_y = padded[1:-1, 2:] - center
    transport = jnp.maximum(speed_x, 0.0) * back_x + jnp.minimum(speed_x, 0.0) * ahead_x
    transport = transport + jnp.maximum(speed_y, 0.0) * back_y + jnp.minimum(speed_y, 0.0) * ahead_y
    return center - time_step * band * transport


def on_device(
    hidden,
    front,
    spectral_weight,
    skip_gain,
    skip_bias,
    project_weight,
    project_bias,
    ice_mask,
    front_flags,
):
    halo = LS_STEPS
    local_chan, row_count, columns = hidden.shape
    row_devices = lax.axis_size("rows")
    chan_devices = lax.axis_size("chan")
    local_ymodes = spectral_weight.shape[1]
    all_rows = row_count * row_devices
    all_xmodes = spectral_weight.shape[2] * chan_devices
    all_ymodes = local_ymodes * row_devices
    tile_cols = columns // chan_devices
    win_rows = row_count + 2 * halo
    norm_scale = 1.0 / math.sqrt(all_rows * columns * all_xmodes * all_ymodes)

    fields = jnp.stack(
        [front, front_flags.astype(jnp.float32), ice_mask.astype(jnp.float32)]
    )

    table = base_table(all_ymodes, columns)
    half = all_xmodes // 2
    if all_rows == columns and all_ymodes > half:
        x_table = table
    else:
        x_table = base_table(half + 1, all_rows)
    x_modes = x_table.shape[0] // 2

    spec_y = jnp.einsum("cxy,ky->ckx", hidden, table, precision=high)
    spec_y = spec_y.reshape(local_chan, 2, all_ymodes, row_count)
    by_freq = lax.all_to_all(spec_y, "rows", split_axis=2, concat_axis=3, tiled=True)
    hidden_late, fields, by_freq = lax.optimization_barrier((hidden, fields, by_freq))
    hidden_win, fields = rows_halo_pair(hidden_late, fields, halo)
    fields = with_halo(fields, (("chan", 2),), halo)
    fields, hidden_win = lax.optimization_barrier((fields, hidden_win))
    parts = jnp.einsum("caqx,kx->caqk", by_freq, x_table, precision=high)
    cos_part = parts[..., :x_modes]
    sin_part = parts[..., x_modes:]
    real_in = unfold_modes(
        cos_part[:, 0] - sin_part[:, 1], cos_part[:, 0] + sin_part[:, 1], half
    )
    imag_in = unfold_modes(
        cos_part[:, 1] + sin_part[:, 0], cos_part[:, 1] - sin_part[:, 0], half
    )
    spectra = jnp.stack([real_in, imag_in], axis=2)

    gathered = lax.all_to_all(spectra, "chan", split_axis=3, concat_axis=0, tiled=True)
    real_in = gathered[:, :, 0]
    imag_in = gathered[:, :, 1]
    real_out = jnp.einsum(
        "qpio,iqp->oqp", spectral_weight[0], real_in, precision=high
    ) - jnp.einsum("qpio,iqp->oqp", spectral_weight[1], imag_in, precision=high)
    imag_out = jnp.einsum(
        "qpio,iqp->oqp", spectral_weight[0], imag_in, precision=high
    ) + jnp.einsum("qpio,iqp->oqp", spectral_weight[1], real_in, precision=high)
    mixed = lax.all_to_all(
        jnp.stack([real_out, imag_out], axis=2), "chan", split_axis=0, concat_axis=3, tiled=True
    )

    real_pos, real_neg = fold_modes(mixed[:, :, 0], half)
    imag_pos, imag_neg = fold_modes(mixed[:, :, 1], half)
    pad = [(0, 0), (0, 0), (0, x_modes - half - 1)]
    coef_real = jnp.concatenate(
        [jnp.pad(real_pos + real_neg, pad), jnp.pad(imag_pos - imag_neg, pad)], axis=-1
    )
    coef_imag = jnp.concatenate(
        [jnp.pad(imag_pos + imag_neg, pad), jnp.pad(real_neg - real_pos, pad)], axis=-1
    )
    coef = jnp.stack([coef_real, coef_imag], axis=1)
    inverted = jnp.einsum("otqk,kx->otqx", coef, x_table, precision=high)
    inverted = windows(inverted, row_devices, row_count, halo)
    inverted = lax.all_to_all(inverted, "rows", split_axis=3, concat_axis=2, tiled=True)
    y_weights = jnp.where(jnp.arange(all_ymodes) == 0, 1.0, 2.0).astype(jnp.float32) * norm_scale
    inverted = inverted.reshape(local_chan, 2, all_ymodes, win_rows) * y_weights[:, None]
    inverted = inverted.reshape(local_chan, 2 * all_ymodes, win_rows)

    spectral = jnp.einsum("ckx,ky->cxy", inverted, table, precision=high)
    activated = jax.nn.gelu(
        spectral + skip_gain[:, None, None] * hidden_win + skip_bias[:, None, None],
        approximate=False,
    )
    partial_speed = jnp.sum(project_weight[:, :, None, None] * activated[None], axis=1)
    sent = windows(partial_speed, chan_devices, tile_cols, halo)
    sent = jnp.moveaxis(sent, 2, 0)
    chunk_shape = sent.shape[1:]
    chunk = math.prod(chunk_shape)
    lanes = 128
    flat_len = -(-chunk // lanes) * lanes
    flat = jnp.pad(sent.reshape(chan_devices, chunk), ((0, 0), (0, flat_len - chunk)))
    flat = flat.reshape(chan_devices, flat_len // lanes, lanes)
    received = lax.all_to_all(flat, "chan", split_axis=0, concat_axis=0, tiled=True)
    speed = jnp.sum(received, axis=0).reshape(-1)[:chunk].reshape(chunk_shape)
    speed = speed + project_bias[:, None, None]
    speed = speed * fields[2][None]
    velocity = speed[:, halo : halo + row_count, halo : halo + tile_cols]

    level = fields[0]
    band = fields[1]
    for level_step in range(LS_STEPS):
        inner = level_step + 1
        rows_end = win_rows - inner
        cols_end = tile_cols + 2 * halo - inner
        level = advance(
            level,
            speed[0, inner:rows_end, inner:cols_end],
            speed[1, inner:rows_end, inner:cols_end],
            band[inner:rows_end, inner:cols_end],
        )
    return (velocity, level)


def solution(mesh):
    return jax.shard_map(
        on_device,
        mesh=mesh,
        in_specs=(
            P("chan", "rows", None),
            P("rows", "chan"),
            P(None, "rows", "chan", None, None),
            P("chan"),
            P("chan"),
            P(None, "chan"),
            P(),
            P("rows", "chan"),
            P("rows", "chan"),
        ),
        out_specs=(P(None, "rows", "chan"), P("rows", "chan")),
        check_vma=False,
    )
```

```python
import math

import jax
import jax.numpy as jnp
from jax import lax
from jax.sharding import PartitionSpec as P

LS_STEPS = 4


time_step = 0.25
highest = lax.Precision.HIGHEST
high = lax.Precision.HIGH


def with_halo(block, sides, width):
    for axis, dim in sides:
        count = lax.axis_size(axis)
        forward = [(i, i + 1) for i in range(count - 1)]
        backward = [(target, source) for source, target in forward]
        low = lax.ppermute(
            lax.slice_in_dim(block, block.shape[dim] - width, None, axis=dim), axis, forward
        )
        high = lax.ppermute(lax.slice_in_dim(block, 0, width, axis=dim), axis, backward)
        block = jnp.concatenate([low, block, high], axis=dim)
    return block


def angles(freqs, places, length):
    product = freqs[:, None] * places[None, :] % length
    return 2.0 * math.pi / length * product.astype(jnp.float32)


def base_table(modes, length):
    lanes = 128 if length % 128 == 0 else length
    ids = jnp.arange(modes, dtype=jnp.int32)
    coarse = angles(ids, jnp.arange(length // lanes, dtype=jnp.int32) * lanes, length)
    fine = angles(ids, jnp.arange(lanes, dtype=jnp.int32), length)
    cos_hi, sin_hi = jnp.cos(coarse)[:, :, None], jnp.sin(coarse)[:, :, None]
    cos_lo, sin_lo = jnp.cos(fine)[:, None, :], jnp.sin(fine)[:, None, :]
    cos_all = (cos_hi * cos_lo - sin_hi * sin_lo).reshape(modes, length)
    sin_all = (sin_hi * cos_lo + cos_hi * sin_lo).reshape(modes, length)
    return jnp.concatenate([cos_all, -sin_all])


def window_table(modes, length, count, size, halo):
    ids = jnp.arange(modes, dtype=jnp.int32)
    coarse = angles(ids, jnp.arange(count, dtype=jnp.int32) * size, length)
    fine = angles(ids, (jnp.arange(size + 2 * halo, dtype=jnp.int32) - halo) % length, length)
    cos_hi, sin_hi = jnp.cos(coarse)[:, :, None], jnp.sin(coarse)[:, :, None]
    cos_lo, sin_lo = jnp.cos(fine)[:, None, :], jnp.sin(fine)[:, None, :]
    cos_all = cos_hi * cos_lo - sin_hi * sin_lo
    sin_all = sin_hi * cos_lo + cos_hi * sin_lo
    return jnp.concatenate([cos_all, -sin_all])


def fold_modes(vec, half):
    pos = jnp.pad(vec[..., :half], [(0, 0)] * (vec.ndim - 1) + [(0, 1)])
    neg = jnp.pad(jnp.flip(vec[..., half:], -1), [(0, 0)] * (vec.ndim - 1) + [(1, 0)])
    return pos, neg


def unfold_modes(plus, minus, half):
    return jnp.concatenate([plus[..., :half], jnp.flip(minus[..., 1 : half + 1], -1)], axis=-1)


def windows(block, count, size, halo):
    padded = jnp.pad(block, [(0, 0)] * (block.ndim - 1) + [(halo, size)])
    lead = block.shape[:-1]
    main = padded[..., : count * size].reshape(lead + (count, size))
    tail = padded[..., size : size + count * size].reshape(lead + (count, size))
    return jnp.concatenate([main, tail[..., : 2 * halo]], axis=-1)


def halo_2d(block, width):
    n_rows = lax.axis_size("rows")
    n_chan = lax.axis_size("chan")

    def shifted(piece, d_row, d_chan):
        pairs = [
            (r * n_chan + c, (r + d_row) * n_chan + c + d_chan)
            for r in range(n_rows)
            for c in range(n_chan)
            if 0 <= r + d_row < n_rows and 0 <= c + d_chan < n_chan
        ]
        return lax.ppermute(piece, ("rows", "chan"), pairs)

    lo, hi = slice(-width, None), slice(0, width)
    every = slice(None)
    parts = {}
    for d_row, rows in ((1, lo), (0, every), (-1, hi)):
        for d_chan, cols in ((1, lo), (0, every), (-1, hi)):
            piece = block[..., rows, cols]
            parts[d_row, d_chan] = piece if d_row == d_chan == 0 else shifted(piece, d_row, d_chan)
    bands = [
        jnp.concatenate([parts[d_row, 1], parts[d_row, 0], parts[d_row, -1]], axis=-1)
        for d_row in (1, 0, -1)
    ]
    return jnp.concatenate(bands, axis=-2)


def rows_halo_pair(first, second, width):
    count = lax.axis_size("rows")
    forward = [(i, i + 1) for i in range(count - 1)]
    backward = [(target, source) for source, target in forward]

    def packed(rows):
        a, b = first[..., rows, :], second[..., rows, :]
        return jnp.concatenate([a.reshape(-1), b.reshape(-1)]), a.shape, b.shape

    def unpacked(flat, a_shape, b_shape):
        split = math.prod(a_shape)
        return flat[:split].reshape(a_shape), flat[split:].reshape(b_shape)

    low, a_shape, b_shape = packed(slice(-width, None))
    high, _, _ = packed(slice(0, width))
    low_a, low_b = unpacked(lax.ppermute(low, "rows", forward), a_shape, b_shape)
    high_a, high_b = unpacked(lax.ppermute(high, "rows", backward), a_shape, b_shape)
    return (
        jnp.concatenate([low_a, first, high_a], axis=-2),
        jnp.concatenate([low_b, second, high_b], axis=-2),
    )


def advance(padded, speed_x, speed_y, band):
    center = padded[1:-1, 1:-1]
    back_x = center - padded[:-2, 1:-1]
    ahead_x = padded[2:, 1:-1] - center
    back_y = center - padded[1:-1, :-2]
    ahead_y = padded[1:-1, 2:] - center
    transport = jnp.maximum(speed_x, 0.0) * back_x + jnp.minimum(speed_x, 0.0) * ahead_x
    transport = transport + jnp.maximum(speed_y, 0.0) * back_y + jnp.minimum(speed_y, 0.0) * ahead_y
    return center - time_step * band * transport


def on_device(
    hidden,
    front,
    spectral_weight,
    skip_gain,
    skip_bias,
    project_weight,
    project_bias,
    ice_mask,
    front_flags,
):
    halo = LS_STEPS
    local_chan, row_count, columns = hidden.shape
    row_devices = lax.axis_size("rows")
    chan_devices = lax.axis_size("chan")
    local_ymodes = spectral_weight.shape[1]
    all_rows = row_count * row_devices
    all_xmodes = spectral_weight.shape[2] * chan_devices
    all_ymodes = local_ymodes * row_devices
    tile_cols = columns // chan_devices
    win_rows = row_count + 2 * halo
    norm_scale = 1.0 / math.sqrt(all_rows * columns * all_xmodes * all_ymodes)

    fields = jnp.stack(
        [front, front_flags.astype(jnp.float32), ice_mask.astype(jnp.float32)]
    )

    table = base_table(all_ymodes, columns)
    half = all_xmodes // 2
    if all_rows == columns and all_ymodes > half:
        x_table = table
    else:
        x_table = base_table(half + 1, all_rows)
    x_modes = x_table.shape[0] // 2

    spec_y = jnp.einsum("cxy,ky->ckx", hidden, table, precision=high)
    spec_y = spec_y.reshape(local_chan, 2, all_ymodes, row_count)
    by_freq = lax.all_to_all(spec_y, "rows", split_axis=2, concat_axis=3, tiled=True)
    hidden_late, fields, by_freq = lax.optimization_barrier((hidden, fields, by_freq))
    hidden_win, fields = rows_halo_pair(hidden_late, fields, halo)
    fields = with_halo(fields, (("chan", 2),), halo)
    fields, hidden_win = lax.optimization_barrier((fields, hidden_win))
    parts = jnp.einsum("caqx,kx->caqk", by_freq, x_table, precision=high)
    cos_part = parts[..., :x_modes]
    sin_part = parts[..., x_modes:]
    real_in = unfold_modes(
        cos_part[:, 0] - sin_part[:, 1], cos_part[:, 0] + sin_part[:, 1], half
    )
    imag_in = unfold_modes(
        cos_part[:, 1] + sin_part[:, 0], cos_part[:, 1] - sin_part[:, 0], half
    )
    spectra = jnp.stack([real_in, imag_in], axis=2)

    gathered = lax.all_to_all(spectra, "chan", split_axis=3, concat_axis=0, tiled=True)
    real_in = gathered[:, :, 0]
    imag_in = gathered[:, :, 1]
    real_out = jnp.einsum(
        "qpio,iqp->oqp", spectral_weight[0], real_in, precision=highest
    ) - jnp.einsum("qpio,iqp->oqp", spectral_weight[1], imag_in, precision=highest)
    imag_out = jnp.einsum(
        "qpio,iqp->oqp", spectral_weight[0], imag_in, precision=highest
    ) + jnp.einsum("qpio,iqp->oqp", spectral_weight[1], real_in, precision=highest)
    mixed = lax.all_to_all(
        jnp.stack([real_out, imag_out], axis=2), "chan", split_axis=0, concat_axis=3, tiled=True
    )

    real_pos, real_neg = fold_modes(mixed[:, :, 0], half)
    imag_pos, imag_neg = fold_modes(mixed[:, :, 1], half)
    pad = [(0, 0), (0, 0), (0, x_modes - half - 1)]
    coef_real = jnp.concatenate(
        [jnp.pad(real_pos + real_neg, pad), jnp.pad(imag_pos - imag_neg, pad)], axis=-1
    )
    coef_imag = jnp.concatenate(
        [jnp.pad(imag_pos + imag_neg, pad), jnp.pad(real_neg - real_pos, pad)], axis=-1
    )
    coef = jnp.stack([coef_real, coef_imag], axis=1)
    row_windows = window_table(x_modes, all_rows, row_devices, row_count, halo)
    inverted = jnp.einsum("otqk,krj->otqrj", coef, row_windows, precision=high)
    inverted = lax.all_to_all(inverted, "rows", split_axis=3, concat_axis=2, tiled=True)
    y_weights = jnp.where(jnp.arange(all_ymodes) == 0, 1.0, 2.0).astype(jnp.float32) * norm_scale
    inverted = inverted.reshape(local_chan, 2, all_ymodes, win_rows) * y_weights[:, None]
    inverted = inverted.reshape(local_chan, 2 * all_ymodes, win_rows)

    spectral = jnp.einsum("ckx,ky->cxy", inverted, table, precision=high)
    activated = jax.nn.gelu(
        spectral + skip_gain[:, None, None] * hidden_win + skip_bias[:, None, None],
        approximate=False,
    )
    partial_speed = jnp.sum(project_weight[:, :, None, None] * activated[None], axis=1)
    sent = windows(partial_speed, chan_devices, tile_cols, halo)
    sent = jnp.moveaxis(sent, 2, 0)
    chunk_shape = sent.shape[1:]
    chunk = math.prod(chunk_shape)
    lanes = 128
    flat_len = -(-chunk // lanes) * lanes
    flat = jnp.pad(sent.reshape(chan_devices, chunk), ((0, 0), (0, flat_len - chunk)))
    flat = flat.reshape(chan_devices, flat_len // lanes, lanes)
    received = lax.all_to_all(flat, "chan", split_axis=0, concat_axis=0, tiled=True)
    speed = jnp.sum(received, axis=0).reshape(-1)[:chunk].reshape(chunk_shape)
    speed = speed + project_bias[:, None, None]
    speed = speed * fields[2][None]
    velocity = speed[:, halo : halo + row_count, halo : halo + tile_cols]

    level = fields[0]
    band = fields[1]
    for level_step in range(LS_STEPS):
        inner = level_step + 1
        rows_end = win_rows - inner
        cols_end = tile_cols + 2 * halo - inner
        level = advance(
            level,
            speed[0, inner:rows_end, inner:cols_end],
            speed[1, inner:rows_end, inner:cols_end],
            band[inner:rows_end, inner:cols_end],
        )
    return (velocity, level)


def solution(mesh):
    return jax.shard_map(
        on_device,
        mesh=mesh,
        in_specs=(
            P("chan", "rows", None),
            P("rows", "chan"),
            P(None, "rows", "chan", None, None),
            P("chan"),
            P("chan"),
            P(None, "chan"),
            P(),
            P("rows", "chan"),
            P("rows", "chan"),
        ),
        out_specs=(P(None, "rows", "chan"), P("rows", "chan")),
        check_vma=False,
    )
```

```python
import math

import jax
import jax.numpy as jnp
from jax import lax
from jax.sharding import PartitionSpec as P

LS_STEPS = 4


time_step = 0.25
highest = lax.Precision.HIGHEST
high = lax.Precision.HIGH


def with_halo(block, sides, width):
    for axis, dim in sides:
        count = lax.axis_size(axis)
        forward = [(i, i + 1) for i in range(count - 1)]
        backward = [(target, source) for source, target in forward]
        low = lax.ppermute(
            lax.slice_in_dim(block, block.shape[dim] - width, None, axis=dim), axis, forward
        )
        high = lax.ppermute(lax.slice_in_dim(block, 0, width, axis=dim), axis, backward)
        block = jnp.concatenate([low, block, high], axis=dim)
    return block


def angles(freqs, places, length):
    product = freqs[:, None] * places[None, :] % length
    return 2.0 * math.pi / length * product.astype(jnp.float32)


def base_table(modes, length):
    lanes = 128 if length % 128 == 0 else length
    ids = jnp.arange(modes, dtype=jnp.int32)
    coarse = angles(ids, jnp.arange(length // lanes, dtype=jnp.int32) * lanes, length)
    fine = angles(ids, jnp.arange(lanes, dtype=jnp.int32), length)
    cos_hi, sin_hi = jnp.cos(coarse)[:, :, None], jnp.sin(coarse)[:, :, None]
    cos_lo, sin_lo = jnp.cos(fine)[:, None, :], jnp.sin(fine)[:, None, :]
    cos_all = (cos_hi * cos_lo - sin_hi * sin_lo).reshape(modes, length)
    sin_all = (sin_hi * cos_lo + cos_hi * sin_lo).reshape(modes, length)
    return jnp.concatenate([cos_all, -sin_all])


def window_table(modes, length, count, size, halo):
    ids = jnp.arange(modes, dtype=jnp.int32)
    coarse = angles(ids, jnp.arange(count, dtype=jnp.int32) * size, length)
    fine = angles(ids, (jnp.arange(size + 2 * halo, dtype=jnp.int32) - halo) % length, length)
    cos_hi, sin_hi = jnp.cos(coarse)[:, :, None], jnp.sin(coarse)[:, :, None]
    cos_lo, sin_lo = jnp.cos(fine)[:, None, :], jnp.sin(fine)[:, None, :]
    cos_all = cos_hi * cos_lo - sin_hi * sin_lo
    sin_all = sin_hi * cos_lo + cos_hi * sin_lo
    return jnp.concatenate([cos_all, -sin_all])


def fold_modes(vec, half):
    pos = jnp.pad(vec[..., :half], [(0, 0)] * (vec.ndim - 1) + [(0, 1)])
    neg = jnp.pad(jnp.flip(vec[..., half:], -1), [(0, 0)] * (vec.ndim - 1) + [(1, 0)])
    return pos, neg


def unfold_modes(plus, minus, half):
    return jnp.concatenate([plus[..., :half], jnp.flip(minus[..., 1 : half + 1], -1)], axis=-1)


def windows(block, count, size, halo):
    padded = jnp.pad(block, [(0, 0)] * (block.ndim - 1) + [(halo, size)])
    lead = block.shape[:-1]
    main = padded[..., : count * size].reshape(lead + (count, size))
    tail = padded[..., size : size + count * size].reshape(lead + (count, size))
    return jnp.concatenate([main, tail[..., : 2 * halo]], axis=-1)


def halo_2d(block, width):
    n_rows = lax.axis_size("rows")
    n_chan = lax.axis_size("chan")

    def shifted(piece, d_row, d_chan):
        pairs = [
            (r * n_chan + c, (r + d_row) * n_chan + c + d_chan)
            for r in range(n_rows)
            for c in range(n_chan)
            if 0 <= r + d_row < n_rows and 0 <= c + d_chan < n_chan
        ]
        return lax.ppermute(piece, ("rows", "chan"), pairs)

    lo, hi = slice(-width, None), slice(0, width)
    every = slice(None)
    parts = {}
    for d_row, rows in ((1, lo), (0, every), (-1, hi)):
        for d_chan, cols in ((1, lo), (0, every), (-1, hi)):
            piece = block[..., rows, cols]
            parts[d_row, d_chan] = piece if d_row == d_chan == 0 else shifted(piece, d_row, d_chan)
    bands = [
        jnp.concatenate([parts[d_row, 1], parts[d_row, 0], parts[d_row, -1]], axis=-1)
        for d_row in (1, 0, -1)
    ]
    return jnp.concatenate(bands, axis=-2)


def rows_halo_pair(first, second, width):
    count = lax.axis_size("rows")
    forward = [(i, i + 1) for i in range(count - 1)]
    backward = [(target, source) for source, target in forward]

    def packed(rows):
        a, b = first[..., rows, :], second[..., rows, :]
        return jnp.concatenate([a.reshape(-1), b.reshape(-1)]), a.shape, b.shape

    def unpacked(flat, a_shape, b_shape):
        split = math.prod(a_shape)
        return flat[:split].reshape(a_shape), flat[split:].reshape(b_shape)

    low, a_shape, b_shape = packed(slice(-width, None))
    high, _, _ = packed(slice(0, width))
    low_a, low_b = unpacked(lax.ppermute(low, "rows", forward), a_shape, b_shape)
    high_a, high_b = unpacked(lax.ppermute(high, "rows", backward), a_shape, b_shape)
    return (
        jnp.concatenate([low_a, first, high_a], axis=-2),
        jnp.concatenate([low_b, second, high_b], axis=-2),
    )


def advance(padded, speed_x, speed_y, band):
    center = padded[1:-1, 1:-1]
    back_x = center - padded[:-2, 1:-1]
    ahead_x = padded[2:, 1:-1] - center
    back_y = center - padded[1:-1, :-2]
    ahead_y = padded[1:-1, 2:] - center
    transport = jnp.maximum(speed_x, 0.0) * back_x + jnp.minimum(speed_x, 0.0) * ahead_x
    transport = transport + jnp.maximum(speed_y, 0.0) * back_y + jnp.minimum(speed_y, 0.0) * ahead_y
    return center - time_step * band * transport


def on_device(
    hidden,
    front,
    spectral_weight,
    skip_gain,
    skip_bias,
    project_weight,
    project_bias,
    ice_mask,
    front_flags,
):
    halo = LS_STEPS
    local_chan, row_count, columns = hidden.shape
    row_devices = lax.axis_size("rows")
    chan_devices = lax.axis_size("chan")
    local_ymodes = spectral_weight.shape[1]
    all_rows = row_count * row_devices
    all_xmodes = spectral_weight.shape[2] * chan_devices
    all_ymodes = local_ymodes * row_devices
    tile_cols = columns // chan_devices
    win_rows = row_count + 2 * halo
    norm_scale = 1.0 / math.sqrt(all_rows * columns * all_xmodes * all_ymodes)

    fields = jnp.stack(
        [front, front_flags.astype(jnp.float32), ice_mask.astype(jnp.float32)]
    )

    table = base_table(all_ymodes, columns)
    half = all_xmodes // 2
    if all_rows == columns and all_ymodes > half:
        x_table = table
    else:
        x_table = base_table(half + 1, all_rows)
    x_modes = x_table.shape[0] // 2

    spec_y = jnp.einsum("cxy,ky->kcx", hidden, table, precision=high)
    spec_y = spec_y.reshape(2, all_ymodes, local_chan, row_count)
    by_freq = lax.all_to_all(spec_y, "rows", split_axis=1, concat_axis=3, tiled=True)
    hidden_late, fields, by_freq = lax.optimization_barrier((hidden, fields, by_freq))
    hidden_win, fields = rows_halo_pair(hidden_late, fields, halo)
    fields = with_halo(fields, (("chan", 2),), halo)
    fields, hidden_win = lax.optimization_barrier((fields, hidden_win))
    parts = jnp.einsum("aqcx,kx->caqk", by_freq, x_table, precision=high)
    cos_part = parts[..., :x_modes]
    sin_part = parts[..., x_modes:]
    real_in = unfold_modes(
        cos_part[:, 0] - sin_part[:, 1], cos_part[:, 0] + sin_part[:, 1], half
    )
    imag_in = unfold_modes(
        cos_part[:, 1] + sin_part[:, 0], cos_part[:, 1] - sin_part[:, 0], half
    )
    spectra = jnp.stack([real_in, imag_in], axis=2)

    gathered = lax.all_to_all(spectra, "chan", split_axis=3, concat_axis=0, tiled=True)
    real_in = gathered[:, :, 0]
    imag_in = gathered[:, :, 1]
    real_out = jnp.einsum(
        "qpio,iqp->oqp", spectral_weight[0], real_in, precision=highest
    ) - jnp.einsum("qpio,iqp->oqp", spectral_weight[1], imag_in, precision=highest)
    imag_out = jnp.einsum(
        "qpio,iqp->oqp", spectral_weight[0], imag_in, precision=highest
    ) + jnp.einsum("qpio,iqp->oqp", spectral_weight[1], real_in, precision=highest)
    mixed = lax.all_to_all(
        jnp.stack([real_out, imag_out], axis=2), "chan", split_axis=0, concat_axis=3, tiled=True
    )

    real_pos, real_neg = fold_modes(mixed[:, :, 0], half)
    imag_pos, imag_neg = fold_modes(mixed[:, :, 1], half)
    pad = [(0, 0), (0, 0), (0, x_modes - half - 1)]
    coef_real = jnp.concatenate(
        [jnp.pad(real_pos + real_neg, pad), jnp.pad(imag_pos - imag_neg, pad)], axis=-1
    )
    coef_imag = jnp.concatenate(
        [jnp.pad(imag_pos + imag_neg, pad), jnp.pad(real_neg - real_pos, pad)], axis=-1
    )
    coef = jnp.stack([coef_real, coef_imag], axis=1)
    row_windows = window_table(x_modes, all_rows, row_devices, row_count, halo)
    inverted = jnp.einsum("otqk,krj->otqrj", coef, row_windows, precision=high)
    inverted = lax.all_to_all(inverted, "rows", split_axis=3, concat_axis=2, tiled=True)
    y_weights = jnp.where(jnp.arange(all_ymodes) == 0, 1.0, 2.0).astype(jnp.float32) * norm_scale
    inverted = inverted.reshape(local_chan, 2, all_ymodes, win_rows) * y_weights[:, None]
    inverted = inverted.reshape(local_chan, 2 * all_ymodes, win_rows)

    spectral = jnp.einsum("ckx,ky->cxy", inverted, table, precision=high)
    activated = jax.nn.gelu(
        spectral + skip_gain[:, None, None] * hidden_win + skip_bias[:, None, None],
        approximate=False,
    )
    partial_speed = jnp.sum(project_weight[:, :, None, None] * activated[None], axis=1)
    sent = windows(partial_speed, chan_devices, tile_cols, halo)
    sent = jnp.moveaxis(sent, 2, 0)
    chunk_shape = sent.shape[1:]
    chunk = math.prod(chunk_shape)
    lanes = 128
    flat_len = -(-chunk // lanes) * lanes
    flat = jnp.pad(sent.reshape(chan_devices, chunk), ((0, 0), (0, flat_len - chunk)))
    flat = flat.reshape(chan_devices, flat_len // lanes, lanes)
    received = lax.all_to_all(flat, "chan", split_axis=0, concat_axis=0, tiled=True)
    speed = jnp.sum(received, axis=0).reshape(-1)[:chunk].reshape(chunk_shape)
    speed = speed + project_bias[:, None, None]
    speed = speed * fields[2][None]
    velocity = speed[:, halo : halo + row_count, halo : halo + tile_cols]

    level = fields[0]
    band = fields[1]
    for level_step in range(LS_STEPS):
        inner = level_step + 1
        rows_end = win_rows - inner
        cols_end = tile_cols + 2 * halo - inner
        level = advance(
            level,
            speed[0, inner:rows_end, inner:cols_end],
            speed[1, inner:rows_end, inner:cols_end],
            band[inner:rows_end, inner:cols_end],
        )
    return (velocity, level)


def solution(mesh):
    return jax.shard_map(
        on_device,
        mesh=mesh,
        in_specs=(
            P("chan", "rows", None),
            P("rows", "chan"),
            P(None, "rows", "chan", None, None),
            P("chan"),
            P("chan"),
            P(None, "chan"),
            P(),
            P("rows", "chan"),
            P("rows", "chan"),
        ),
        out_specs=(P(None, "rows", "chan"), P("rows", "chan")),
        check_vma=False,
    )
```

```python
import math

import jax
import jax.numpy as jnp
from jax import lax
from jax.sharding import PartitionSpec as P

LS_STEPS = 4


time_step = 0.25
highest = lax.Precision.HIGHEST
high = lax.Precision.HIGH


def with_halo(block, sides, width):
    for axis, dim in sides:
        count = lax.axis_size(axis)
        forward = [(i, i + 1) for i in range(count - 1)]
        backward = [(target, source) for source, target in forward]
        low = lax.ppermute(
            lax.slice_in_dim(block, block.shape[dim] - width, None, axis=dim), axis, forward
        )
        high = lax.ppermute(lax.slice_in_dim(block, 0, width, axis=dim), axis, backward)
        block = jnp.concatenate([low, block, high], axis=dim)
    return block


def angles(freqs, places, length):
    product = freqs[:, None] * places[None, :] % length
    return 2.0 * math.pi / length * product.astype(jnp.float32)


def base_table(modes, length):
    lanes = 128 if length % 128 == 0 else length
    ids = jnp.arange(modes, dtype=jnp.int32)
    coarse = angles(ids, jnp.arange(length // lanes, dtype=jnp.int32) * lanes, length)
    fine = angles(ids, jnp.arange(lanes, dtype=jnp.int32), length)
    cos_hi, sin_hi = jnp.cos(coarse)[:, :, None], jnp.sin(coarse)[:, :, None]
    cos_lo, sin_lo = jnp.cos(fine)[:, None, :], jnp.sin(fine)[:, None, :]
    cos_all = (cos_hi * cos_lo - sin_hi * sin_lo).reshape(modes, length)
    sin_all = (sin_hi * cos_lo + cos_hi * sin_lo).reshape(modes, length)
    return jnp.concatenate([cos_all, -sin_all])


def window_table(modes, length, count, size, halo):
    ids = jnp.arange(modes, dtype=jnp.int32)
    coarse = angles(ids, jnp.arange(count, dtype=jnp.int32) * size, length)
    fine = angles(ids, (jnp.arange(size + 2 * halo, dtype=jnp.int32) - halo) % length, length)
    cos_hi, sin_hi = jnp.cos(coarse)[:, :, None], jnp.sin(coarse)[:, :, None]
    cos_lo, sin_lo = jnp.cos(fine)[:, None, :], jnp.sin(fine)[:, None, :]
    cos_all = cos_hi * cos_lo - sin_hi * sin_lo
    sin_all = sin_hi * cos_lo + cos_hi * sin_lo
    return jnp.concatenate([cos_all, -sin_all])


def fold_modes(vec, half):
    pos = jnp.pad(vec[..., :half], [(0, 0)] * (vec.ndim - 1) + [(0, 1)])
    neg = jnp.pad(jnp.flip(vec[..., half:], -1), [(0, 0)] * (vec.ndim - 1) + [(1, 0)])
    return pos, neg


def unfold_modes(plus, minus, half):
    return jnp.concatenate([plus[..., :half], jnp.flip(minus[..., 1 : half + 1], -1)], axis=-1)


def windows(block, count, size, halo):
    padded = jnp.pad(block, [(0, 0)] * (block.ndim - 1) + [(halo, size)])
    lead = block.shape[:-1]
    main = padded[..., : count * size].reshape(lead + (count, size))
    tail = padded[..., size : size + count * size].reshape(lead + (count, size))
    return jnp.concatenate([main, tail[..., : 2 * halo]], axis=-1)


def halo_2d(block, width):
    n_rows = lax.axis_size("rows")
    n_chan = lax.axis_size("chan")

    def shifted(piece, d_row, d_chan):
        pairs = [
            (r * n_chan + c, (r + d_row) * n_chan + c + d_chan)
            for r in range(n_rows)
            for c in range(n_chan)
            if 0 <= r + d_row < n_rows and 0 <= c + d_chan < n_chan
        ]
        return lax.ppermute(piece, ("rows", "chan"), pairs)

    lo, hi = slice(-width, None), slice(0, width)
    every = slice(None)
    parts = {}
    for d_row, rows in ((1, lo), (0, every), (-1, hi)):
        for d_chan, cols in ((1, lo), (0, every), (-1, hi)):
            piece = block[..., rows, cols]
            parts[d_row, d_chan] = piece if d_row == d_chan == 0 else shifted(piece, d_row, d_chan)
    bands = [
        jnp.concatenate([parts[d_row, 1], parts[d_row, 0], parts[d_row, -1]], axis=-1)
        for d_row in (1, 0, -1)
    ]
    return jnp.concatenate(bands, axis=-2)


def rows_halo_pair(first, second, width):
    count = lax.axis_size("rows")
    forward = [(i, i + 1) for i in range(count - 1)]
    backward = [(target, source) for source, target in forward]

    def packed(rows):
        a, b = first[..., rows, :], second[..., rows, :]
        return jnp.concatenate([a.reshape(-1), b.reshape(-1)]), a.shape, b.shape

    def unpacked(flat, a_shape, b_shape):
        split = math.prod(a_shape)
        return flat[:split].reshape(a_shape), flat[split:].reshape(b_shape)

    low, a_shape, b_shape = packed(slice(-width, None))
    high, _, _ = packed(slice(0, width))
    low_a, low_b = unpacked(lax.ppermute(low, "rows", forward), a_shape, b_shape)
    high_a, high_b = unpacked(lax.ppermute(high, "rows", backward), a_shape, b_shape)
    return (
        jnp.concatenate([low_a, first, high_a], axis=-2),
        jnp.concatenate([low_b, second, high_b], axis=-2),
    )


def advance(padded, speed_x, speed_y, band):
    center = padded[1:-1, 1:-1]
    back_x = center - padded[:-2, 1:-1]
    ahead_x = padded[2:, 1:-1] - center
    back_y = center - padded[1:-1, :-2]
    ahead_y = padded[1:-1, 2:] - center
    transport = jnp.maximum(speed_x, 0.0) * back_x + jnp.minimum(speed_x, 0.0) * ahead_x
    transport = transport + jnp.maximum(speed_y, 0.0) * back_y + jnp.minimum(speed_y, 0.0) * ahead_y
    return center - time_step * band * transport


def on_device(
    hidden,
    front,
    spectral_weight,
    skip_gain,
    skip_bias,
    project_weight,
    project_bias,
    ice_mask,
    front_flags,
):
    halo = LS_STEPS
    local_chan, row_count, columns = hidden.shape
    row_devices = lax.axis_size("rows")
    chan_devices = lax.axis_size("chan")
    local_ymodes = spectral_weight.shape[1]
    all_rows = row_count * row_devices
    all_xmodes = spectral_weight.shape[2] * chan_devices
    all_ymodes = local_ymodes * row_devices
    tile_cols = columns // chan_devices
    win_rows = row_count + 2 * halo
    norm_scale = 1.0 / math.sqrt(all_rows * columns * all_xmodes * all_ymodes)

    fields = jnp.stack(
        [front, front_flags.astype(jnp.float32), ice_mask.astype(jnp.float32)]
    )

    table = base_table(all_ymodes, columns)
    half = all_xmodes // 2
    if all_rows == columns and all_ymodes > half:
        x_table = table
    else:
        x_table = base_table(half + 1, all_rows)
    x_modes = x_table.shape[0] // 2

    spec_y = jnp.einsum("cxy,ky->kcx", hidden, table, precision=high)
    spec_y = spec_y.reshape(2, all_ymodes, local_chan, row_count)
    by_freq = lax.all_to_all(spec_y, "rows", split_axis=1, concat_axis=3, tiled=True)
    hidden_late, fields, by_freq = lax.optimization_barrier((hidden, fields, by_freq))
    hidden_win, fields = rows_halo_pair(hidden_late, fields, halo)
    fields = with_halo(fields, (("chan", 2),), halo)
    fields, hidden_win = lax.optimization_barrier((fields, hidden_win))
    parts = jnp.einsum("aqcx,kx->caqk", by_freq, x_table, precision=high)
    cos_part = parts[..., :x_modes]
    sin_part = parts[..., x_modes:]
    real_in = unfold_modes(
        cos_part[:, 0] - sin_part[:, 1], cos_part[:, 0] + sin_part[:, 1], half
    )
    imag_in = unfold_modes(
        cos_part[:, 1] + sin_part[:, 0], cos_part[:, 1] - sin_part[:, 0], half
    )
    spectra = jnp.stack([real_in, imag_in], axis=2)

    gathered = lax.all_to_all(spectra, "chan", split_axis=3, concat_axis=0, tiled=True)
    real_in = gathered[:, :, 0]
    imag_in = gathered[:, :, 1]
    real_out = jnp.einsum(
        "qpio,iqp->oqp", spectral_weight[0], real_in, precision=highest
    ) - jnp.einsum("qpio,iqp->oqp", spectral_weight[1], imag_in, precision=highest)
    imag_out = jnp.einsum(
        "qpio,iqp->oqp", spectral_weight[0], imag_in, precision=highest
    ) + jnp.einsum("qpio,iqp->oqp", spectral_weight[1], real_in, precision=highest)
    mixed = lax.all_to_all(
        jnp.stack([real_out, imag_out], axis=2), "chan", split_axis=0, concat_axis=3, tiled=True
    )

    real_pos, real_neg = fold_modes(mixed[:, :, 0], half)
    imag_pos, imag_neg = fold_modes(mixed[:, :, 1], half)
    pad = [(0, 0), (0, 0), (0, x_modes - half - 1)]
    coef_real = jnp.concatenate(
        [jnp.pad(real_pos + real_neg, pad), jnp.pad(imag_pos - imag_neg, pad)], axis=-1
    )
    coef_imag = jnp.concatenate(
        [jnp.pad(imag_pos + imag_neg, pad), jnp.pad(real_neg - real_pos, pad)], axis=-1
    )
    coef = jnp.stack([coef_real, coef_imag], axis=1)
    row_windows = window_table(x_modes, all_rows, row_devices, row_count, halo)
    inverted = jnp.einsum("otqk,krj->rotqj", coef, row_windows, precision=high)
    inverted = lax.all_to_all(inverted, "rows", split_axis=0, concat_axis=3, tiled=True)
    y_weights = jnp.where(jnp.arange(all_ymodes) == 0, 1.0, 2.0).astype(jnp.float32) * norm_scale
    inverted = inverted.reshape(local_chan, 2, all_ymodes, win_rows) * y_weights[:, None]
    inverted = inverted.reshape(local_chan, 2 * all_ymodes, win_rows)

    spectral = jnp.einsum("ckx,ky->cxy", inverted, table, precision=high)
    activated = jax.nn.gelu(
        spectral + skip_gain[:, None, None] * hidden_win + skip_bias[:, None, None],
        approximate=False,
    )
    partial_speed = jnp.sum(project_weight[:, :, None, None] * activated[None], axis=1)
    sent = windows(partial_speed, chan_devices, tile_cols, halo)
    sent = jnp.moveaxis(sent, 2, 0)
    chunk_shape = sent.shape[1:]
    chunk = math.prod(chunk_shape)
    lanes = 128
    flat_len = -(-chunk // lanes) * lanes
    flat = jnp.pad(sent.reshape(chan_devices, chunk), ((0, 0), (0, flat_len - chunk)))
    flat = flat.reshape(chan_devices, flat_len // lanes, lanes)
    received = lax.all_to_all(flat, "chan", split_axis=0, concat_axis=0, tiled=True)
    speed = jnp.sum(received, axis=0).reshape(-1)[:chunk].reshape(chunk_shape)
    speed = speed + project_bias[:, None, None]
    speed = speed * fields[2][None]
    velocity = speed[:, halo : halo + row_count, halo : halo + tile_cols]

    level = fields[0]
    band = fields[1]
    for level_step in range(LS_STEPS):
        inner = level_step + 1
        rows_end = win_rows - inner
        cols_end = tile_cols + 2 * halo - inner
        level = advance(
            level,
            speed[0, inner:rows_end, inner:cols_end],
            speed[1, inner:rows_end, inner:cols_end],
            band[inner:rows_end, inner:cols_end],
        )
    return (velocity, level)


def solution(mesh):
    return jax.shard_map(
        on_device,
        mesh=mesh,
        in_specs=(
            P("chan", "rows", None),
            P("rows", "chan"),
            P(None, "rows", "chan", None, None),
            P("chan"),
            P("chan"),
            P(None, "chan"),
            P(),
            P("rows", "chan"),
            P("rows", "chan"),
        ),
        out_specs=(P(None, "rows", "chan"), P("rows", "chan")),
        check_vma=False,
    )
```
